32 devices in a mesh: grp: 8 (over z, y), band: 4 (over x, core).
Axes of the slice: x: 2, y: 2, z: 4, core: 2. Of those that a mesh axis runs over, the one named last changes fastest.
Arguments:
- x_blocks: bfloat16 [4, 4, 64, 8192], P('band', None, None, 'grp'), may hold values from -6 to 6
- pair_ids: int32 [8, 4, 4], P('grp', 'band'), may hold values from 0 to 15, as said below
- live_count: int32 [8, 4], P('grp', 'band'), may hold values from 2 to 4, as said below
- green_occ: bfloat16 [512, 512], replicated, may hold values from -0.0234375 to 0.0234375
- green_virt: bfloat16 [512, 512], replicated, may hold values from -0.0234375 to 0.0234375
Outputs:
- chi: float32 [128, 128], P(('grp', 'band'))
The draws below stay inside these ranges and needn't reach their ends.
Inputs may be any that keep to these rules, and one draw needn't show every extreme that they name: On each device the 4 codes pair_ids[g, b, :] are distinct; code e names mu block e // 2 and nu block 2 * b + e % 2. `live_count`: in every draw some device has all 4 slots live.
All inputs are finite; a program needn't handle non-finite values.
Results may differ from the reference program's by a relative error of at most 0.0041.
Values may be sent and summed in bfloat16 or wider, within the bound.
No kernel may reach another device: no remote copies, remote signals or barrier semaphores. Data moves between devices by JAX's collectives and lax.ppermute only.
A program may use at most 128 MiB of HBM per device.

```python
import jax
import jax.numpy as jnp
from jax import lax

BLK = 64
P_DEV = 16
GROUPS = 8
BANDS = 4
OWN = 128
NORB = 512
NP = 128
SLOTS = 4


def pair_tables(key):
    perm_key = jax.random.fold_in(key, 11)
    first_key = jax.random.fold_in(key, 12)
    second_key = jax.random.fold_in(key, 13)
    pick_key = jax.random.fold_in(key, 14)
    device_keys = jax.random.split(perm_key, GROUPS * BANDS)
    orders = jax.vmap(lambda one_key: jax.random.permutation(one_key, 4 * BANDS))(device_keys)
    codes = orders[:, :SLOTS].reshape(GROUPS, BANDS, SLOTS).astype(jnp.int32)
    first = jax.random.randint(first_key, (GROUPS * BANDS,), 2, SLOTS + 1)
    second = jax.random.randint(second_key, (GROUPS * BANDS,), 2, SLOTS + 1)
    counts = jnp.minimum(first, second)
    chosen = jax.random.randint(pick_key, (), 0, GROUPS * BANDS)
    positions = jnp.arange(GROUPS * BANDS, dtype=jnp.int32)
    counts = jnp.where(positions == chosen, SLOTS, counts)
    return (codes, counts.reshape(GROUPS, BANDS).astype(jnp.int32))


def draw_pair_ids(key, part):
    return pair_tables(key)[0]


def draw_live_count(key, part):
    return pair_tables(key)[1]


def shard_levels(stream_key, extent, cuts, smallest, high):
    def one(position, blocks):
        draws = jax.random.uniform(jax.random.fold_in(jax.random.fold_in(stream_key, 6), position), (blocks,), jnp.float32, smallest / len(cuts), high / len(cuts))
        return jnp.repeat(jnp.exp(draws), extent[position] // blocks).reshape((-1,) + (1,) * (len(extent) - position - 1))

    gain = one(*cuts[0])
    for cut in cuts[1:]:
        gain = gain * one(*cut)
    return gain


def normal_values(key, extent, deviation, limit, shards=(), kind=jnp.bfloat16):
    array = jax.random.normal(key, extent, jnp.float32) * deviation
    if len(shards) > 0:
        array = shard_levels(key, extent, shards, -0.22, 0.18) * array
    return jnp.clip(array, min=-limit, max=limit).astype(kind)


def setup_inputs(seed: int = 0) -> dict:
    key_of = jax.random.split(jax.random.key(seed), 6)
    x_blocks = normal_values(key_of[0], (BANDS, SLOTS, BLK, NP * BLK), 1.0, 6.0, ((0, 4), (3, 8)))
    pair_ids = draw_pair_ids(jax.random.fold_in(key_of[5], 71), 0)
    live_count = draw_live_count(jax.random.fold_in(key_of[5], 71), 0)
    green_occ = normal_values(key_of[3], (NORB, NORB), (4 * SLOTS * BLK * BLK) ** -0.5, 0.0234375)
    green_virt = normal_values(key_of[4], (NORB, NORB), (4 * SLOTS * BLK * BLK) ** -0.5, 0.0234375)
    return dict(x_blocks=x_blocks, pair_ids=pair_ids, live_count=live_count, green_occ=green_occ, green_virt=green_virt)


def occ_piece(slabs, pair_list, live_slots, green_cols):
    ri_local = slabs.shape[2] // BLK
    col_count = green_cols.shape[1]

    def add_slot(slot, total):
        pair_code = pair_list[slot]
        mu_block = pair_code // 2
        half_index = pair_code % 2
        rows = lax.dynamic_slice_in_dim(green_cols, mu_block * BLK, BLK, 0)
        term = lax.dot_general(slabs[slot], rows, (((0,), (0,)), ((), ())), preferred_element_type=jnp.float32)
        term = jnp.where(slot < live_slots, term, 0.0).reshape(ri_local, 1, BLK, col_count)
        current = lax.dynamic_slice_in_dim(total, half_index, 1, 1)
        return lax.dynamic_update_slice_in_dim(total, current + term, half_index, 1)

    start = jnp.zeros((ri_local, 2, BLK, col_count), jnp.float32)
    total = lax.fori_loop(0, SLOTS, add_slot, start)
    return total.reshape(ri_local, 2 * BLK, col_count)


def virt_piece(slabs, pair_list, live_slots, green):
    ri_local = slabs.shape[2] // BLK
    orbitals = green.shape[1]

    def add_slot(slot, total):
        pair_code = pair_list[slot]
        mu_block = pair_code // 2
        half_index = pair_code % 2
        rows = lax.dynamic_slice_in_dim(green, mu_block * BLK, BLK, 0)
        term = lax.dot_general(rows, slabs[slot], (((0,), (0,)), ((), ())), preferred_element_type=jnp.float32)
        term = jnp.where(slot < live_slots, term, 0.0).reshape(orbitals, ri_local, 1, BLK)
        current = lax.dynamic_slice_in_dim(total, half_index, 1, 2)
        return lax.dynamic_update_slice_in_dim(total, current + term, half_index, 2)

    start = jnp.zeros((orbitals, ri_local, 2, BLK), jnp.float32)
    total = lax.fori_loop(0, SLOTS, add_slot, start)
    return total.reshape(orbitals, ri_local, 2 * BLK)


def reference(x_blocks, pair_ids, live_count, green_occ, green_virt):
    blocks_all = jnp.moveaxis(x_blocks.reshape(BANDS, SLOTS, BLK, GROUPS, P_DEV * BLK), 3, 0)
    occ_map = jax.vmap(jax.vmap(occ_piece, in_axes=(0, 0, 0, None)), in_axes=(0, 0, 0, None))
    virt_map = jax.vmap(virt_piece, in_axes=(0, 0, 0, None))

    def band_term(response, band_index):
        green_cols = lax.dynamic_slice_in_dim(green_occ, band_index * OWN, OWN, 1)
        occ_three = occ_map(blocks_all, pair_ids, live_count, green_cols).astype(jnp.bfloat16)
        occ_three = jnp.transpose(occ_three, (0, 2, 1, 3, 4)).reshape(NP, NORB, OWN)
        band_blocks = lax.dynamic_index_in_dim(blocks_all, band_index, 1, keepdims=False)
        band_pairs = lax.dynamic_index_in_dim(pair_ids, band_index, 1, keepdims=False)
        band_live = lax.dynamic_index_in_dim(live_count, band_index, 1, keepdims=False)
        virt_three = virt_map(band_blocks, band_pairs, band_live, green_virt).astype(jnp.bfloat16)
        virt_three = jnp.transpose(virt_three, (1, 0, 2, 3)).reshape(NORB, NP, OWN)
        term = lax.dot_general(occ_three.astype(jnp.float32), virt_three.astype(jnp.float32),
                               (((1, 2), (0, 2)), ((), ())), precision=lax.Precision.HIGHEST)
        return response + term, None

    response, unused = lax.scan(band_term, jnp.zeros((NP, NP), jnp.float32), jnp.arange(BANDS, dtype=jnp.int32))
    return response
```

```python
import jax
import jax.numpy as jnp
from jax import lax
from jax.sharding import PartitionSpec as P


def slot_weights(pair_list, live_slots, slot_count):
    slot_index = jnp.arange(slot_count, dtype=jnp.int32)
    live = slot_index[None, :] < live_slots[:, None]
    halves = pair_list % 2
    rows = [jnp.logical_and(live, halves == h) for h in range(2)]
    return jnp.stack(rows, axis=1).astype(jnp.bfloat16)


def block_rows(green, pair_list, block_size):
    mu_blocks = pair_list // 2
    row_index = mu_blocks[..., None] * block_size + jnp.arange(block_size, dtype=jnp.int32)
    taken = jnp.take(green, row_index.reshape(-1), axis=0)
    return taken.reshape(pair_list.shape + (block_size, green.shape[1]))


def on_device(x_blocks, pair_ids, live_count, green_occ, green_virt):
    local_blocks = x_blocks[0]
    slot_count, block_size, ri_cols = local_blocks.shape
    ri_local = ri_cols // block_size
    orbitals = green_occ.shape[0]
    band_orbs = 2 * block_size
    band_count = lax.axis_size("band")
    group_count = lax.axis_size("grp")
    band = lax.axis_index("band")

    pair_list = pair_ids[0, 0]
    live_slots = live_count[0, 0]

    xg = lax.all_gather(local_blocks, "band")
    pg = lax.all_gather(pair_list, "band")
    lg = lax.all_gather(live_slots, "band")
    xb = lax.all_gather(local_blocks, "grp")
    pb = lax.all_gather(pair_list, "grp")
    lb = lax.all_gather(live_slots, "grp")

    occ_cols = lax.dynamic_slice_in_dim(green_occ, band * band_orbs, band_orbs, 1)
    occ_rows = block_rows(occ_cols, pg, block_size)
    wg = slot_weights(pg, lg, slot_count)
    occ_sel = occ_rows[:, None] * wg[:, :, :, None, None]
    xg_r = xg.reshape(band_count, slot_count, block_size, ri_local, block_size)
    occ_three = jnp.einsum(
        "bsipj,bhsil->pbhjl", xg_r, occ_sel, preferred_element_type=jnp.float32
    ).astype(jnp.bfloat16)
    occ_three = occ_three.reshape(ri_local, orbitals, band_orbs)

    wb = slot_weights(pb, lb, slot_count)
    xb_r = xb.reshape(group_count, slot_count, block_size, ri_local, block_size)

    def one_group(carry, item):
        x_one, p_one, w_one = item
        virt_rows = block_rows(green_virt, p_one, block_size)
        virt_sel = virt_rows[None] * w_one[:, :, None, None]
        virt_three = jnp.einsum(
            "hsin,siqj->qnhj", virt_sel, x_one, preferred_element_type=jnp.float32
        ).astype(jnp.bfloat16)
        virt_three = virt_three.reshape(ri_local, orbitals, band_orbs)
        part = lax.dot_general(
            occ_three, virt_three, (((1, 2), (1, 2)), ((), ())),
            preferred_element_type=jnp.float32,
        )
        return carry, part

    unused, parts = lax.scan(one_group, 0, (xb_r, pb, wb))
    partial_value = jnp.transpose(parts, (1, 0, 2)).reshape(ri_local, group_count * ri_local)
    response = lax.psum_scatter(partial_value, "band", scatter_dimension=0, tiled=True)
    return response


def solution(mesh):
    placed = (P("band", None, None, "grp"), P("grp", "band", None), P("grp", "band"), P(), P())
    return jax.shard_map(
        on_device, mesh=mesh, in_specs=placed, out_specs=P(("grp", "band"), None), check_vma=False
    )
```

```python
import jax
import jax.numpy as jnp
from jax import lax
from jax.sharding import PartitionSpec as P

META = 128


def on_device(x_blocks, pair_ids, live_count, green_occ, green_virt):
    local_blocks = x_blocks[0]
    slot_count, block_size, ri_cols = local_blocks.shape
    ri_local = ri_cols // block_size
    orbitals = green_occ.shape[0]
    band_orbs = 2 * block_size
    band_count = lax.axis_size("band")
    group_count = lax.axis_size("grp")
    band = lax.axis_index("band")
    flat = slot_count * block_size * block_size
    code_count = 2 * (orbitals // block_size)

    pair_list = pair_ids[0, 0]
    live_slots = live_count[0, 0]

    live = (jnp.arange(slot_count, dtype=jnp.int32) < live_slots).astype(local_blocks.dtype)
    masked = local_blocks * live[:, None, None]
    xt = masked.reshape(slot_count, block_size, ri_local, block_size)
    xt = jnp.transpose(xt, (2, 0, 3, 1)).reshape(ri_local, flat)
    meta = jnp.zeros((ri_local, META), local_blocks.dtype)
    meta = meta.at[0, :slot_count].set(pair_list.astype(local_blocks.dtype))
    packed = jnp.concatenate([xt, meta], axis=1)

    xg = lax.all_gather(packed, "band")
    xb = lax.all_gather(packed, "grp")
    codes_g = xg[:, 0, flat:flat + slot_count].astype(jnp.float32).astype(jnp.int32)
    codes_b = xb[:, 0, flat:flat + slot_count].astype(jnp.float32).astype(jnp.int32)

    occ_cols = lax.dynamic_slice_in_dim(green_occ, band * band_orbs, band_orbs, 1)
    row_index = (codes_g // 2)[..., None] * block_size + jnp.arange(block_size, dtype=jnp.int32)
    occ_rows = jnp.take(occ_cols, row_index.reshape(-1), axis=0)
    occ_rows = occ_rows.reshape(band_count, slot_count, block_size, band_orbs)
    halves = (codes_g % 2)[:, None, :] == jnp.arange(2, dtype=jnp.int32)[None, :, None]
    occ_sel = occ_rows[:, None] * halves.astype(occ_rows.dtype)[..., None, None]
    xg_x = xg[:, :, :flat].reshape(band_count, ri_local, slot_count, block_size, block_size)
    occ_three = jnp.einsum(
        "bpsji,bhsil->plbhj", xg_x, occ_sel, preferred_element_type=jnp.float32
    ).astype(jnp.bfloat16)
    occ_three = occ_three.reshape(ri_local, band_orbs, orbitals)

    folded = lax.dot_general(
        occ_three, green_virt, (((2,), (1,)), ((), ())), preferred_element_type=jnp.float32
    )
    folded = folded.reshape(ri_local, 2, block_size, orbitals // block_size, block_size)
    folded = jnp.transpose(folded, (0, 3, 1, 2, 4)).reshape(ri_local, code_count, block_size * block_size)

    xb_x = xb[:, :, :flat]
    chunk = max(1, min(group_count, (8 << 20) // (ri_local * flat * 4)))
    while group_count % chunk:
        chunk -= 1

    def one_chunk(item):
        x_part, code_part = item
        sel = jnp.take(folded, code_part.reshape(-1), axis=1)
        sel = sel.reshape(ri_local, chunk, flat)
        return jnp.einsum(
            "pgk,gqk->gpq", sel, x_part.astype(jnp.float32),
            precision=lax.Precision.HIGHEST, preferred_element_type=jnp.float32,
        )

    steps = group_count // chunk
    if steps == 1:
        parts = one_chunk((xb_x, codes_b))
    else:
        parts = lax.map(
            one_chunk,
            (xb_x.reshape(steps, chunk, ri_local, flat), codes_b.reshape(steps, chunk, slot_count)),
        ).reshape(group_count, ri_local, ri_local)
    partial_value = jnp.transpose(parts, (1, 0, 2)).reshape(ri_local, group_count * ri_local)
    response = lax.psum_scatter(partial_value, "band", scatter_dimension=0, tiled=True)
    return response


def solution(mesh):
    placed = (P("band", None, None, "grp"), P("grp", "band", None), P("grp", "band"), P(), P())
    return jax.shard_map(
        on_device, mesh=mesh, in_specs=placed, out_specs=P(("grp", "band"), None), check_vma=False
    )
```

```python
import jax
import jax.numpy as jnp
from jax import lax
from jax.sharding import PartitionSpec as P

META = 128


def snake(count):
    half = count // 2
    return [2 * o for o in range(half)] + [2 * o + 1 for o in reversed(range(half))]


def ring_gather(buf, axis, count):
    order = snake(count)
    pos_of = [order.index(d) for d in range(count)]
    fwd = [(order[k], order[(k + 1) % count]) for k in range(count)]
    bwd = [(order[k], order[(k - 1) % count]) for k in range(count)]
    me = lax.axis_index(axis)
    pos = jnp.array(pos_of, jnp.int32)[me]
    order_arr = jnp.array(order, jnp.int32)
    got = [(me, buf)]
    ahead = behind = buf
    for step in range(1, count // 2):
        ahead = lax.ppermute(ahead, axis, fwd)
        behind = lax.ppermute(behind, axis, bwd)
        got.append((order_arr[(pos - step) % count], ahead))
        got.append((order_arr[(pos + step) % count], behind))
    rows = buf.shape[0] // 2
    first = lax.ppermute(ahead[:rows], axis, fwd)
    second = lax.ppermute(behind[rows:], axis, bwd)
    got.append((order_arr[(pos + count // 2) % count], jnp.concatenate([first, second], axis=0)))
    return got


def on_device(x_blocks, pair_ids, live_count, green_occ, green_virt):
    local_blocks = x_blocks[0]
    slot_count, block_size, ri_cols = local_blocks.shape
    ri_local = ri_cols // block_size
    orbitals = green_occ.shape[0]
    band_orbs = 2 * block_size
    band_count = lax.axis_size("band")
    group_count = lax.axis_size("grp")
    band = lax.axis_index("band")
    flat = slot_count * block_size * block_size
    code_count = 2 * (orbitals // block_size)

    pair_list = pair_ids[0, 0]
    live_slots = live_count[0, 0]

    live = (jnp.arange(slot_count, dtype=jnp.int32) < live_slots).astype(local_blocks.dtype)
    masked = local_blocks * live[:, None, None]
    xt = masked.reshape(slot_count, block_size, ri_local, block_size)
    xt = jnp.transpose(xt, (2, 0, 3, 1)).reshape(ri_local, flat)
    meta = jnp.zeros((ri_local, META), local_blocks.dtype)
    meta = meta.at[0, :slot_count].set(pair_list.astype(local_blocks.dtype))
    packed = jnp.concatenate([xt, meta], axis=1)

    band_got = ring_gather(packed, "band", band_count)
    band_ids = jnp.stack([src for src, unused in band_got])
    xg = jnp.stack([buf for unused, buf in band_got])
    codes_g = xg[:, 0, flat:flat + slot_count].astype(jnp.float32).astype(jnp.int32)
    grp_got = ring_gather(packed, "grp", group_count)

    occ_cols = lax.dynamic_slice_in_dim(green_occ, band * band_orbs, band_orbs, 1)
    row_index = (codes_g // 2)[..., None] * block_size + jnp.arange(block_size, dtype=jnp.int32)
    occ_rows = jnp.take(occ_cols, row_index.reshape(-1), axis=0)
    occ_rows = occ_rows.reshape(band_count, slot_count, block_size, band_orbs)
    halves = (codes_g % 2)[:, None, :] == jnp.arange(2, dtype=jnp.int32)[None, :, None]
    occ_sel = occ_rows[:, None] * halves.astype(occ_rows.dtype)[..., None, None]
    xg_x = xg[:, :, :flat].reshape(band_count, ri_local, slot_count, block_size, block_size)
    occ_three = jnp.einsum(
        "bpsji,bhsil->plbhj", xg_x, occ_sel, preferred_element_type=jnp.float32
    ).astype(jnp.bfloat16)
    occ_three = occ_three.reshape(ri_local, band_orbs, orbitals)

    col_index = (band_ids[:, None] * band_orbs + jnp.arange(band_orbs, dtype=jnp.int32)).reshape(-1)
    virt_cols = jnp.take(green_virt, col_index, axis=1)
    folded = lax.dot_general(
        occ_three, virt_cols, (((2,), (1,)), ((), ())), preferred_element_type=jnp.float32
    )
    folded = folded.reshape(ri_local, 2, block_size, orbitals // block_size, block_size)
    folded = jnp.transpose(folded, (0, 3, 1, 2, 4)).reshape(ri_local, code_count, block_size * block_size)

    fold_hi = folded.astype(jnp.bfloat16)
    fold_lo = (folded - fold_hi.astype(jnp.float32)).astype(jnp.bfloat16)

    partial_value = jnp.zeros((ri_local, group_count * ri_local), jnp.float32)
    for src, buf in grp_got:
        codes = buf[0, flat:flat + slot_count].astype(jnp.float32).astype(jnp.int32)
        x_part = buf[:, :flat]
        part = jnp.zeros((ri_local, ri_local), jnp.float32)
        for table in (fold_hi, fold_lo):
            sel = jnp.take(table, codes, axis=1).reshape(ri_local, flat)
            part = part + lax.dot_general(
                sel, x_part, (((1,), (1,)), ((), ())), preferred_element_type=jnp.float32
            )
        partial_value = lax.dynamic_update_slice_in_dim(partial_value, part, src * ri_local, 1)
    response = lax.psum_scatter(partial_value, "band", scatter_dimension=0, tiled=True)
    return response


def solution(mesh):
    placed = (P("band", None, None, "grp"), P("grp", "band", None), P("grp", "band"), P(), P())
    return jax.shard_map(
        on_device, mesh=mesh, in_specs=placed, out_specs=P(("grp", "band"), None), check_vma=False
    )
```

```python
import jax
import jax.numpy as jnp
from jax import lax
from jax.experimental import pallas as pl
from jax.experimental.pallas import tpu as pltpu
from jax.sharding import PartitionSpec as P

META = 128


def snake(count):
    half = count // 2
    return [2 * o for o in range(half)] + [2 * o + 1 for o in reversed(range(half))]


def ring_gather(buf, axis, count):
    order = snake(count)
    pos_of = [order.index(d) for d in range(count)]
    fwd = [(order[k], order[(k + 1) % count]) for k in range(count)]
    bwd = [(order[k], order[(k - 1) % count]) for k in range(count)]
    me = lax.axis_index(axis)
    pos = jnp.array(pos_of, jnp.int32)[me]
    order_arr = jnp.array(order, jnp.int32)
    got = [(me, buf)]
    ahead = behind = buf
    for step in range(1, count // 2):
        ahead = lax.ppermute(ahead, axis, fwd)
        behind = lax.ppermute(behind, axis, bwd)
        got.append((order_arr[(pos - step) % count], ahead))
        got.append((order_arr[(pos + step) % count], behind))
    rows = buf.shape[0] // 2
    first = lax.ppermute(ahead[:rows], axis, fwd)
    second = lax.ppermute(behind[rows:], axis, bwd)
    got.append((order_arr[(pos + count // 2) % count], jnp.concatenate([first, second], axis=0)))
    return got


def contract_kernel(codes_ref, hi_ref, lo_ref, x_ref, out_ref, *, slots, width):
    g = pl.program_id(0)
    acc = jnp.zeros(out_ref.shape[1:], jnp.float32)
    for s in range(slots):
        code = codes_ref[g, s]
        xs = x_ref[0, :, s * width:(s + 1) * width]
        for table in (hi_ref, lo_ref):
            acc = acc + lax.dot_general(
                table[code], xs, (((1,), (1,)), ((), ())), preferred_element_type=jnp.float32
            )
    out_ref[0] = acc


def contract(codes, table_hi, table_lo, xstack, slots, width):
    groups, rows, unused = xstack.shape
    codes_total, ri, unused = table_hi.shape
    table_spec = pl.BlockSpec((codes_total, ri, width), lambda g, c: (0, 0, 0))
    grid_spec = pltpu.PrefetchScalarGridSpec(
        num_scalar_prefetch=1,
        grid=(groups,),
        in_specs=[table_spec, table_spec, pl.BlockSpec((1, rows, slots * width), lambda g, c: (g, 0, 0))],
        out_specs=pl.BlockSpec((1, ri, rows), lambda g, c: (g, 0, 0)),
    )
    body = lambda *refs: contract_kernel(*refs, slots=slots, width=width)
    return pl.pallas_call(
        body, out_shape=jax.ShapeDtypeStruct((groups, ri, rows), jnp.float32), grid_spec=grid_spec
    )(codes, table_hi, table_lo, xstack)


def on_device(x_blocks, pair_ids, live_count, green_occ, green_virt):
    local_blocks = x_blocks[0]
    slot_count, block_size, ri_cols = local_blocks.shape
    ri_local = ri_cols // block_size
    orbitals = green_occ.shape[0]
    band_orbs = 2 * block_size
    band_count = lax.axis_size("band")
    group_count = lax.axis_size("grp")
    band = lax.axis_index("band")
    flat = slot_count * block_size * block_size
    code_count = 2 * (orbitals // block_size)

    pair_list = pair_ids[0, 0]
    live_slots = live_count[0, 0]

    live = (jnp.arange(slot_count, dtype=jnp.int32) < live_slots).astype(local_blocks.dtype)
    masked = local_blocks * live[:, None, None]
    xt = masked.reshape(slot_count, block_size, ri_local, block_size)
    xt = jnp.transpose(xt, (2, 0, 3, 1)).reshape(ri_local, flat)
    meta = jnp.zeros((ri_local, META), local_blocks.dtype)
    meta = meta.at[0, :slot_count].set(pair_list.astype(local_blocks.dtype))
    packed = jnp.concatenate([xt, meta], axis=1)

    rows2d = masked.reshape(slot_count * block_size, ri_cols)
    meta_rows = jnp.zeros((16, ri_cols), local_blocks.dtype)
    meta_rows = meta_rows.at[0, :slot_count].set(pair_list.astype(local_blocks.dtype))
    band_packed = jnp.concatenate([rows2d, meta_rows], axis=0)
    band_got = ring_gather(band_packed, "band", band_count)
    band_ids = jnp.stack([src for src, unused in band_got])
    xg = jnp.stack([buf for unused, buf in band_got])
    kdim = slot_count * block_size
    codes_g = xg[:, kdim, :slot_count].astype(jnp.float32).astype(jnp.int32)
    grp_got = ring_gather(packed, "grp", group_count)

    occ_cols = lax.dynamic_slice_in_dim(green_occ, band * band_orbs, band_orbs, 1)
    row_index = (codes_g // 2)[..., None] * block_size + jnp.arange(block_size, dtype=jnp.int32)
    occ_rows = jnp.take(occ_cols, row_index.reshape(-1), axis=0)
    occ_rows = occ_rows.reshape(band_count, slot_count, block_size, band_orbs)
    halves = (codes_g % 2)[:, None, :] == jnp.arange(2, dtype=jnp.int32)[None, :, None]
    occ_sel = occ_rows[:, None] * halves.astype(occ_rows.dtype)[..., None, None]
    occ_sel = occ_sel.reshape(band_count, 2, kdim, band_orbs)
    occ_raw = jnp.einsum(
        "bkr,bhkl->bhrl", xg[:, :kdim, :], occ_sel, preferred_element_type=jnp.float32
    ).astype(jnp.bfloat16)
    occ_raw = occ_raw.reshape(band_count, 2, ri_local, block_size, band_orbs)
    occ_three = jnp.transpose(occ_raw, (2, 4, 0, 1, 3)).reshape(ri_local, band_orbs, orbitals)

    col_index = (band_ids[:, None] * band_orbs + jnp.arange(band_orbs, dtype=jnp.int32)).reshape(-1)
    virt_cols = jnp.take(green_virt, col_index, axis=1)
    folded = lax.dot_general(
        occ_three, virt_cols, (((2,), (1,)), ((), ())), preferred_element_type=jnp.float32
    )
    folded = folded.reshape(ri_local, 2, block_size, orbitals // block_size, block_size)
    folded = jnp.transpose(folded, (0, 3, 1, 2, 4)).reshape(ri_local, code_count, block_size * block_size)

    fold_hi = lax.reduce_precision(folded, exponent_bits=8, mantissa_bits=7)
    fold_lo = (folded - fold_hi).astype(jnp.bfloat16)
    fold_hi = fold_hi.astype(jnp.bfloat16)
    fold_hi = jnp.transpose(fold_hi, (1, 0, 2))
    fold_lo = jnp.transpose(fold_lo, (1, 0, 2))

    grp_ids = jnp.stack([src for src, unused in grp_got])
    xstack = jnp.stack([buf for unused, buf in grp_got])
    codes_b = xstack[:, 0, flat:flat + slot_count].astype(jnp.float32).astype(jnp.int32)
    parts = contract(codes_b, fold_hi, fold_lo, xstack, slot_count, block_size * block_size)
    order = jnp.zeros((group_count,), jnp.int32).at[grp_ids].set(jnp.arange(group_count, dtype=jnp.int32))
    parts = jnp.take(parts, order, axis=0)
    partial_value = jnp.transpose(parts, (1, 0, 2)).reshape(ri_local, group_count * ri_local)
    response = lax.psum_scatter(partial_value, "band", scatter_dimension=0, tiled=True)
    return response


def solution(mesh):
    placed = (P("band", None, None, "grp"), P("grp", "band", None), P("grp", "band"), P(), P())
    return jax.shard_map(
        on_device, mesh=mesh, in_specs=placed, out_specs=P(("grp", "band"), None), check_vma=False
    )
```

```python
import jax
import jax.numpy as jnp
from jax import lax
from jax.experimental import pallas as pl
from jax.experimental.pallas import tpu as pltpu
from jax.sharding import PartitionSpec as P

META = 128


def snake(count):
    half = count // 2
    return [2 * o for o in range(half)] + [2 * o + 1 for o in reversed(range(half))]


def ring_gather(buf, axis, count):
    order = snake(count)
    pos_of = [order.index(d) for d in range(count)]
    fwd = [(order[k], order[(k + 1) % count]) for k in range(count)]
    bwd = [(order[k], order[(k - 1) % count]) for k in range(count)]
    me = lax.axis_index(axis)
    pos = jnp.array(pos_of, jnp.int32)[me]
    order_arr = jnp.array(order, jnp.int32)
    got = [(me, buf)]
    ahead = behind = buf
    for step in range(1, count // 2):
        ahead = lax.ppermute(ahead, axis, fwd)
        behind = lax.ppermute(behind, axis, bwd)
        got.append((order_arr[(pos - step) % count], ahead))
        got.append((order_arr[(pos + step) % count], behind))
    rows = buf.shape[0] // 2
    first = lax.ppermute(ahead[:rows], axis, fwd)
    second = lax.ppermute(behind[rows:], axis, bwd)
    got.append((order_arr[(pos + count // 2) % count], jnp.concatenate([first, second], axis=0)))
    return got


def contract_kernel(codes_ref, hi_ref, lo_ref, x_ref, out_ref, *, slots, width):
    g = pl.program_id(0)
    acc = jnp.zeros(out_ref.shape[1:], jnp.float32)
    for s in range(slots):
        code = codes_ref[g, s]
        xs = x_ref[0, :, s * width:(s + 1) * width]
        for table in (hi_ref, lo_ref):
            acc = acc + lax.dot_general(
                table[code], xs, (((1,), (1,)), ((), ())), preferred_element_type=jnp.float32
            )
    out_ref[0] = acc


def contract(codes, table_hi, table_lo, xstack, slots, width):
    groups, rows, unused = xstack.shape
    codes_total, ri, unused = table_hi.shape
    table_spec = pl.BlockSpec((codes_total, ri, width), lambda g, c: (0, 0, 0))
    grid_spec = pltpu.PrefetchScalarGridSpec(
        num_scalar_prefetch=1,
        grid=(groups,),
        in_specs=[table_spec, table_spec, pl.BlockSpec((1, rows, slots * width), lambda g, c: (g, 0, 0))],
        out_specs=pl.BlockSpec((1, ri, rows), lambda g, c: (g, 0, 0)),
    )
    body = lambda *refs: contract_kernel(*refs, slots=slots, width=width)
    return pl.pallas_call(
        body, out_shape=jax.ShapeDtypeStruct((groups, ri, rows), jnp.float32), grid_spec=grid_spec
    )(codes, table_hi, table_lo, xstack)


def on_device(x_blocks, pair_ids, live_count, green_occ, green_virt):
    local_blocks = x_blocks[0]
    slot_count, block_size, ri_cols = local_blocks.shape
    ri_local = ri_cols // block_size
    orbitals = green_occ.shape[0]
    band_orbs = 2 * block_size
    band_count = lax.axis_size("band")
    group_count = lax.axis_size("grp")
    band = lax.axis_index("band")
    flat = slot_count * block_size * block_size
    code_count = 2 * (orbitals // block_size)

    pair_list = pair_ids[0, 0]
    live_slots = live_count[0, 0]

    live = (jnp.arange(slot_count, dtype=jnp.int32) < live_slots).astype(local_blocks.dtype)
    masked = local_blocks * live[:, None, None]
    xt = masked.reshape(slot_count, block_size, ri_local, block_size)
    xt = jnp.transpose(xt, (2, 0, 3, 1)).reshape(ri_local, flat)
    meta = jnp.zeros((ri_local, META), local_blocks.dtype)
    meta = meta.at[0, :slot_count].set(pair_list.astype(local_blocks.dtype))
    packed = jnp.concatenate([xt, meta], axis=1)

    rows2d = masked.reshape(slot_count, block_size, ri_local, block_size)
    rows2d = jnp.transpose(rows2d, (0, 1, 3, 2)).reshape(slot_count * block_size, ri_cols)
    meta_rows = jnp.zeros((16, ri_cols), local_blocks.dtype)
    meta_rows = meta_rows.at[0, :slot_count].set(pair_list.astype(local_blocks.dtype))
    band_packed = jnp.concatenate([rows2d, meta_rows], axis=0)
    band_got = ring_gather(band_packed, "band", band_count)
    band_ids = jnp.stack([src for src, unused in band_got])
    xg = jnp.stack([buf for unused, buf in band_got])
    kdim = slot_count * block_size
    codes_g = xg[:, kdim, :slot_count].astype(jnp.float32).astype(jnp.int32)
    grp_got = ring_gather(packed, "grp", group_count)

    occ_cols = lax.dynamic_slice_in_dim(green_occ, band * band_orbs, band_orbs, 1)
    row_index = (codes_g // 2)[..., None] * block_size + jnp.arange(block_size, dtype=jnp.int32)
    occ_rows = jnp.take(occ_cols, row_index.reshape(-1), axis=0)
    occ_rows = occ_rows.reshape(band_count, slot_count, block_size, band_orbs)
    halves = (codes_g % 2)[:, None, :] == jnp.arange(2, dtype=jnp.int32)[None, :, None]
    occ_sel = occ_rows[:, None] * halves.astype(occ_rows.dtype)[..., None, None]
    occ_sel = occ_sel.reshape(band_count, 2, kdim, band_orbs)
    occ_raw = jnp.einsum(
        "bkr,bhkl->bhrl", xg[:, :kdim, :], occ_sel, preferred_element_type=jnp.float32
    ).astype(jnp.bfloat16)
    occ_raw = occ_raw.reshape(band_count, 2, block_size, ri_local, band_orbs)

    virt_cols = jnp.concatenate(
        [lax.dynamic_slice_in_dim(green_virt, band_ids[k] * band_orbs, band_orbs, 1) for k in range(band_count)],
        axis=1,
    ).reshape(orbitals, band_count, 2, block_size)
    folded = lax.dot_general(
        occ_raw, virt_cols, (((0, 1, 2), (1, 2, 3)), ((), ())), preferred_element_type=jnp.float32
    )
    fold_hi = lax.reduce_precision(folded, exponent_bits=8, mantissa_bits=7)
    fold_lo = (folded - fold_hi).astype(jnp.bfloat16)
    fold_hi = fold_hi.astype(jnp.bfloat16)

    def table(part):
        part = part.reshape(ri_local, 2, block_size, orbitals // block_size, block_size)
        part = jnp.transpose(part, (3, 1, 0, 2, 4))
        return part.reshape(code_count, ri_local, block_size * block_size)

    fold_hi = table(fold_hi)
    fold_lo = table(fold_lo)

    grp_ids = jnp.stack([src for src, unused in grp_got])
    xstack = jnp.stack([buf for unused, buf in grp_got])
    codes_b = xstack[:, 0, flat:flat + slot_count].astype(jnp.float32).astype(jnp.int32)
    parts = contract(codes_b, fold_hi, fold_lo, xstack, slot_count, block_size * block_size)
    order = jnp.zeros((group_count,), jnp.int32).at[grp_ids].set(jnp.arange(group_count, dtype=jnp.int32))
    parts = jnp.take(parts, order, axis=0)
    partial_value = jnp.transpose(parts, (1, 0, 2)).reshape(ri_local, group_count * ri_local)
    response = lax.psum_scatter(partial_value, "band", scatter_dimension=0, tiled=True)
    return response


def solution(mesh):
    placed = (P("band", None, None, "grp"), P("grp", "band", None), P("grp", "band"), P(), P())
    return jax.shard_map(
        on_device, mesh=mesh, in_specs=placed, out_specs=P(("grp", "band"), None), check_vma=False
    )
```

```python
import jax
import jax.numpy as jnp
from jax import lax
from jax.experimental import pallas as pl
from jax.experimental.pallas import tpu as pltpu
from jax.sharding import PartitionSpec as P

META = 128


def snake(count):
    half = count // 2
    return [2 * o for o in range(half)] + [2 * o + 1 for o in reversed(range(half))]


def ring_gather(buf, axis, count):
    order = snake(count)
    pos_of = [order.index(d) for d in range(count)]
    fwd = [(order[k], order[(k + 1) % count]) for k in range(count)]
    bwd = [(order[k], order[(k - 1) % count]) for k in range(count)]
    me = lax.axis_index(axis)
    pos = jnp.array(pos_of, jnp.int32)[me]
    order_arr = jnp.array(order, jnp.int32)
    got = [(me, buf)]
    ahead = behind = buf
    for step in range(1, count // 2):
        ahead = lax.ppermute(ahead, axis, fwd)
        behind = lax.ppermute(behind, axis, bwd)
        got.append((order_arr[(pos - step) % count], ahead))
        got.append((order_arr[(pos + step) % count], behind))
    rows = buf.shape[0] // 2
    first = lax.ppermute(ahead[:rows], axis, fwd)
    second = lax.ppermute(behind[rows:], axis, bwd)
    got.append((order_arr[(pos + count // 2) % count], jnp.concatenate([first, second], axis=0)))
    return got


def contract_kernel(codes_ref, hi_ref, lo_ref, x_ref, out_ref, *, slots, width):
    g = pl.program_id(0)
    acc = jnp.zeros(out_ref.shape[1:], jnp.float32)
    for s in range(slots):
        code = codes_ref[g, s]
        xs = x_ref[0, :, s * width:(s + 1) * width]
        for table in (hi_ref, lo_ref):
            acc = acc + lax.dot_general(
                table[code], xs, (((1,), (1,)), ((), ())), preferred_element_type=jnp.float32
            )
    out_ref[0] = acc


def contract(codes, table_hi, table_lo, xstack, slots, width):
    groups, rows, unused = xstack.shape
    codes_total, ri, unused = table_hi.shape
    table_spec = pl.BlockSpec((codes_total, ri, width), lambda g, c: (0, 0, 0))
    grid_spec = pltpu.PrefetchScalarGridSpec(
        num_scalar_prefetch=1,
        grid=(groups,),
        in_specs=[table_spec, table_spec, pl.BlockSpec((1, rows, slots * width), lambda g, c: (g, 0, 0))],
        out_specs=pl.BlockSpec((1, ri, rows), lambda g, c: (g, 0, 0)),
    )
    body = lambda *refs: contract_kernel(*refs, slots=slots, width=width)
    return pl.pallas_call(
        body, out_shape=jax.ShapeDtypeStruct((groups, ri, rows), jnp.float32), grid_spec=grid_spec
    )(codes, table_hi, table_lo, xstack)


def on_device(x_blocks, pair_ids, live_count, green_occ, green_virt):
    local_blocks = x_blocks[0]
    slot_count, block_size, ri_cols = local_blocks.shape
    ri_local = ri_cols // block_size
    orbitals = green_occ.shape[0]
    band_orbs = 2 * block_size
    band_count = lax.axis_size("band")
    group_count = lax.axis_size("grp")
    band = lax.axis_index("band")
    flat = slot_count * block_size * block_size
    code_count = 2 * (orbitals // block_size)

    pair_list = pair_ids[0, 0]
    live_slots = live_count[0, 0]

    live = (jnp.arange(slot_count, dtype=jnp.int32) < live_slots).astype(local_blocks.dtype)
    masked = local_blocks * live[:, None, None]
    xt = masked.reshape(slot_count, block_size, ri_local, block_size)
    xt = jnp.transpose(xt, (2, 0, 3, 1)).reshape(ri_local, flat)
    meta = jnp.zeros((ri_local, META), local_blocks.dtype)
    meta = meta.at[0, :slot_count].set(pair_list.astype(local_blocks.dtype))
    packed = jnp.concatenate([xt, meta], axis=1)

    rows2d = masked.reshape(slot_count, block_size, ri_local, block_size)
    rows2d = jnp.transpose(rows2d, (0, 1, 3, 2)).reshape(slot_count * block_size, ri_cols)
    meta_rows = jnp.zeros((16, ri_cols), local_blocks.dtype)
    meta_rows = meta_rows.at[0, :slot_count].set(pair_list.astype(local_blocks.dtype))
    band_packed = jnp.concatenate([rows2d, meta_rows], axis=0)
    band_got = ring_gather(band_packed, "band", band_count)
    band_ids = jnp.stack([src for src, unused in band_got])
    xg = jnp.stack([buf for unused, buf in band_got])
    kdim = slot_count * block_size
    codes_g = xg[:, kdim, :slot_count].astype(jnp.float32).astype(jnp.int32)
    grp_got = ring_gather(packed, "grp", group_count)
    early = [buf for unused, buf in grp_got[3:5]]
    xg, *early = lax.optimization_barrier([xg] + early)
    grp_got[3:5] = [(src, buf) for (src, unused), buf in zip(grp_got[3:5], early)]

    occ_cols = lax.dynamic_slice_in_dim(green_occ, band * band_orbs, band_orbs, 1)
    row_index = (codes_g // 2)[..., None] * block_size + jnp.arange(block_size, dtype=jnp.int32)
    occ_rows = jnp.take(occ_cols, row_index.reshape(-1), axis=0)
    occ_rows = occ_rows.reshape(band_count, slot_count, block_size, band_orbs)
    halves = (codes_g % 2)[:, None, :] == jnp.arange(2, dtype=jnp.int32)[None, :, None]
    occ_sel = occ_rows[:, None] * halves.astype(occ_rows.dtype)[..., None, None]
    occ_sel = occ_sel.reshape(band_count, 2, kdim, band_orbs)
    occ_raw = jnp.einsum(
        "bkr,bhkl->bhrl", xg[:, :kdim, :], occ_sel, preferred_element_type=jnp.float32
    ).astype(jnp.bfloat16)
    occ_raw = occ_raw.reshape(band_count, 2, block_size, ri_local, band_orbs)
    later = [buf for unused, buf in grp_got[5:7]]
    occ_raw, *later = lax.optimization_barrier([occ_raw] + later)
    grp_got[5:7] = [(src, buf) for (src, unused), buf in zip(grp_got[5:7], later)]

    virt_cols = jnp.concatenate(
        [lax.dynamic_slice_in_dim(green_virt, band_ids[k] * band_orbs, band_orbs, 1) for k in range(band_count)],
        axis=1,
    ).reshape(orbitals, band_count, 2, block_size)
    folded = lax.dot_general(
        occ_raw, virt_cols, (((0, 1, 2), (1, 2, 3)), ((), ())), preferred_element_type=jnp.float32
    )
    folded = folded.reshape(ri_local, 2, block_size, orbitals // block_size, block_size)
    folded = jnp.transpose(folded, (3, 1, 0, 2, 4)).reshape(code_count, ri_local, block_size * block_size)
    fold_hi = lax.reduce_precision(folded, exponent_bits=8, mantissa_bits=7)
    fold_lo = (folded - fold_hi).astype(jnp.bfloat16)
    fold_hi = fold_hi.astype(jnp.bfloat16)

    grp_ids = jnp.stack([src for src, unused in grp_got])
    xstack = jnp.stack([buf for unused, buf in grp_got])
    codes_b = xstack[:, 0, flat:flat + slot_count].astype(jnp.float32).astype(jnp.int32)
    parts = contract(codes_b, fold_hi, fold_lo, xstack, slot_count, block_size * block_size)
    order = jnp.zeros((group_count,), jnp.int32).at[grp_ids].set(jnp.arange(group_count, dtype=jnp.int32))
    parts = jnp.take(parts, order, axis=0)
    partial_value = jnp.transpose(parts, (1, 0, 2)).reshape(ri_local, group_count * ri_local)
    response = lax.psum_scatter(partial_value, "band", scatter_dimension=0, tiled=True)
    return response


def solution(mesh):
    placed = (P("band", None, None, "grp"), P("grp", "band", None), P("grp", "band"), P(), P())
    return jax.shard_map(
        on_device, mesh=mesh, in_specs=placed, out_specs=P(("grp", "band"), None), check_vma=False
    )
```

```python
import jax
import jax.numpy as jnp
from jax import lax
from jax.experimental import pallas as pl
from jax.experimental.pallas import tpu as pltpu
from jax.sharding import PartitionSpec as P

META = 128


def snake(count):
    half = count // 2
    return [2 * o for o in range(half)] + [2 * o + 1 for o in reversed(range(half))]


def ring_gather(buf, axis, count):
    order = snake(count)
    pos_of = [order.index(d) for d in range(count)]
    fwd = [(order[k], order[(k + 1) % count]) for k in range(count)]
    bwd = [(order[k], order[(k - 1) % count]) for k in range(count)]
    me = lax.axis_index(axis)
    pos = jnp.array(pos_of, jnp.int32)[me]
    order_arr = jnp.array(order, jnp.int32)
    shifts = [0]
    got = [buf]
    ahead = behind = buf
    for step in range(1, count // 2):
        ahead = lax.ppermute(ahead, axis, fwd)
        behind = lax.ppermute(behind, axis, bwd)
        got += [ahead, behind]
        shifts += [-step, step]
    rows = buf.shape[0] // 2
    first = lax.ppermute(ahead[:rows], axis, fwd)
    second = lax.ppermute(behind[rows:], axis, bwd)
    got.append(jnp.concatenate([first, second], axis=0))
    shifts.append(count // 2)
    sources = order_arr[(pos + jnp.array(shifts, jnp.int32)) % count]
    return sources, got


def contract_kernel(codes_ref, hi_ref, lo_ref, x_ref, out_ref, *, slots, width):
    g = pl.program_id(0)
    acc = jnp.zeros(out_ref.shape[1:], jnp.float32)
    for s in range(slots):
        code = codes_ref[g, s]
        xs = x_ref[0, :, s * width:(s + 1) * width]
        for table in (hi_ref, lo_ref):
            acc = acc + lax.dot_general(
                table[code], xs, (((1,), (1,)), ((), ())), preferred_element_type=jnp.float32
            )
    out_ref[0] = acc


def contract(codes, table_hi, table_lo, xstack, slots, width):
    groups, rows, unused = xstack.shape
    codes_total, ri, unused = table_hi.shape
    table_spec = pl.BlockSpec((codes_total, ri, width), lambda g, c: (0, 0, 0))
    grid_spec = pltpu.PrefetchScalarGridSpec(
        num_scalar_prefetch=1,
        grid=(groups,),
        in_specs=[table_spec, table_spec, pl.BlockSpec((1, rows, slots * width), lambda g, c: (g, 0, 0))],
        out_specs=pl.BlockSpec((1, ri, rows), lambda g, c: (g, 0, 0)),
    )
    body = lambda *refs: contract_kernel(*refs, slots=slots, width=width)
    return pl.pallas_call(
        body, out_shape=jax.ShapeDtypeStruct((groups, ri, rows), jnp.float32), grid_spec=grid_spec
    )(codes, table_hi, table_lo, xstack)


def on_device(x_blocks, pair_ids, live_count, green_occ, green_virt):
    local_blocks = x_blocks[0]
    slot_count, block_size, ri_cols = local_blocks.shape
    ri_local = ri_cols // block_size
    orbitals = green_occ.shape[0]
    band_orbs = 2 * block_size
    band_count = lax.axis_size("band")
    group_count = lax.axis_size("grp")
    band = lax.axis_index("band")
    flat = slot_count * block_size * block_size
    code_count = 2 * (orbitals // block_size)

    pair_list = pair_ids[0, 0]
    live_slots = live_count[0, 0]

    live = (jnp.arange(slot_count, dtype=jnp.int32) < live_slots).astype(local_blocks.dtype)
    masked = local_blocks * live[:, None, None]
    xt = masked.reshape(slot_count, block_size, ri_local, block_size)
    xt = jnp.transpose(xt, (2, 0, 3, 1)).reshape(ri_local, flat)
    meta = jnp.zeros((ri_local, META), local_blocks.dtype)
    meta = meta.at[0, :slot_count].set(pair_list.astype(local_blocks.dtype))
    packed = jnp.concatenate([xt, meta], axis=1)

    rows2d = masked.reshape(slot_count, block_size, ri_local, block_size)
    rows2d = jnp.transpose(rows2d, (0, 1, 3, 2)).reshape(slot_count * block_size, ri_cols)
    meta_rows = jnp.zeros((16, ri_cols), local_blocks.dtype)
    meta_rows = meta_rows.at[0, :slot_count].set(pair_list.astype(local_blocks.dtype))
    band_packed = jnp.concatenate([rows2d, meta_rows], axis=0)
    band_ids, band_got = ring_gather(band_packed, "band", band_count)
    xg = jnp.stack(band_got)
    kdim = slot_count * block_size
    codes_g = xg[:, kdim, :slot_count].astype(jnp.float32).astype(jnp.int32)
    grp_ids, grp_got = ring_gather(packed, "grp", group_count)
    xg, *early = lax.optimization_barrier([xg] + grp_got[3:5])
    grp_got[3:5] = early

    occ_cols = lax.dynamic_slice_in_dim(green_occ, band * band_orbs, band_orbs, 1)
    row_index = (codes_g // 2)[..., None] * block_size + jnp.arange(block_size, dtype=jnp.int32)
    occ_rows = jnp.take(occ_cols, row_index.reshape(-1), axis=0)
    occ_rows = occ_rows.reshape(band_count, slot_count, block_size, band_orbs)
    halves = (codes_g % 2)[:, None, :] == jnp.arange(2, dtype=jnp.int32)[None, :, None]
    occ_sel = occ_rows[:, None] * halves.astype(occ_rows.dtype)[..., None, None]
    occ_sel = occ_sel.reshape(band_count, 2, kdim, band_orbs)
    occ_raw = jnp.einsum(
        "bkr,bhkl->bhrl", xg[:, :kdim, :], occ_sel, preferred_element_type=jnp.float32
    ).astype(jnp.bfloat16)
    occ_raw = occ_raw.reshape(band_count, 2, block_size, ri_local, band_orbs)
    occ_raw, *later = lax.optimization_barrier([occ_raw] + grp_got[5:7])
    grp_got[5:7] = later

    virt_cols = jnp.concatenate(
        [lax.dynamic_slice_in_dim(green_virt, band_ids[k] * band_orbs, band_orbs, 1) for k in range(band_count)],
        axis=1,
    ).reshape(orbitals, band_count, 2, block_size)
    folded = lax.dot_general(
        occ_raw, virt_cols, (((0, 1, 2), (1, 2, 3)), ((), ())), preferred_element_type=jnp.float32
    )
    folded = lax.optimization_barrier(folded)
    folded = folded.reshape(ri_local, 2, block_size, orbitals // block_size, block_size)
    folded = jnp.transpose(folded, (3, 1, 0, 2, 4)).reshape(code_count, ri_local, block_size * block_size)
    fold_hi = lax.reduce_precision(folded, exponent_bits=8, mantissa_bits=7)
    fold_lo = (folded - fold_hi).astype(jnp.bfloat16)
    fold_hi = fold_hi.astype(jnp.bfloat16)

    xstack = jnp.stack(grp_got)
    codes_b = xstack[:, 0, flat:flat + slot_count].astype(jnp.float32).astype(jnp.int32)
    parts = contract(codes_b, fold_hi, fold_lo, xstack, slot_count, block_size * block_size)
    order = jnp.zeros((group_count,), jnp.int32).at[grp_ids].set(jnp.arange(group_count, dtype=jnp.int32))
    parts = jnp.take(parts, order, axis=0)
    partial_value = jnp.transpose(parts, (1, 0, 2)).reshape(ri_local, group_count * ri_local)
    response = lax.psum_scatter(partial_value, "band", scatter_dimension=0, tiled=True)
    return response


def solution(mesh):
    placed = (P("band", None, None, "grp"), P("grp", "band", None), P("grp", "band"), P(), P())
    return jax.shard_map(
        on_device, mesh=mesh, in_specs=placed, out_specs=P(("grp", "band"), None), check_vma=False
    )
```

```python
import jax
import jax.numpy as jnp
from jax import lax
from jax.experimental import pallas as pl
from jax.experimental.pallas import tpu as pltpu
from jax.sharding import PartitionSpec as P

META = 128


def snake(count):
    half = count // 2
    return [2 * o for o in range(half)] + [2 * o + 1 for o in reversed(range(half))]


def ring_gather(buf, axis, count):
    order = snake(count)
    pos_of = [order.index(d) for d in range(count)]
    fwd = [(order[k], order[(k + 1) % count]) for k in range(count)]
    bwd = [(order[k], order[(k - 1) % count]) for k in range(count)]
    me = lax.axis_index(axis)
    pos = jnp.array(pos_of, jnp.int32)[me]
    order_arr = jnp.array(order, jnp.int32)
    shifts = [0]
    got = [buf]
    ahead = behind = buf
    for step in range(1, count // 2):
        ahead = lax.ppermute(ahead, axis, fwd)
        behind = lax.ppermute(behind, axis, bwd)
        got += [ahead, behind]
        shifts += [-step, step]
    rows = buf.shape[0] // 2
    first = lax.ppermute(ahead[:rows], axis, fwd)
    second = lax.ppermute(behind[rows:], axis, bwd)
    got.append(jnp.concatenate([first, second], axis=0))
    shifts.append(count // 2)
    sources = order_arr[(pos + jnp.array(shifts, jnp.int32)) % count]
    return sources, got


def contract_kernel(codes_ref, table_ref, x_ref, out_ref, hi_ref, lo_ref, dense_ref, *, slots, width, ri, chunk):
    step = pl.program_id(0)

    @pl.when(step == 0)
    def split():
        full = table_ref[...]
        hi = full.astype(jnp.bfloat16)
        hi_ref[...] = hi
        lo_ref[...] = (full - hi.astype(jnp.float32)).astype(jnp.bfloat16)

    out_ref[...] = jnp.zeros(out_ref.shape, jnp.float32)
    for s in range(slots):
        xs = x_ref[:, s * width:(s + 1) * width]
        dense = lax.dot_general(
            hi_ref[...], xs, (((1,), (1,)), ((), ())), preferred_element_type=jnp.float32
        )
        dense = dense + lax.dot_general(
            lo_ref[...], xs, (((1,), (1,)), ((), ())), preferred_element_type=jnp.float32
        )
        dense_ref[...] = dense
        for c in range(chunk):
            code = codes_ref[step * chunk + c, s]
            start = pl.multiple_of(code * ri, ri)
            out_ref[0, :, c * ri:(c + 1) * ri] += dense_ref[pl.ds(start, ri), c * ri:(c + 1) * ri]


def contract(codes, table, xrows, groups, slots, width):
    codes_total, ri, unused = table.shape
    flat = slots * width
    chunk = groups
    while chunk > 1 and (chunk * ri * flat * 2 > (4 << 20) or groups % chunk):
        chunk -= 1
    steps = groups // chunk
    table2 = table.reshape(codes_total * ri, width)
    grid_spec = pltpu.PrefetchScalarGridSpec(
        num_scalar_prefetch=1,
        grid=(steps,),
        in_specs=[
            pl.BlockSpec((codes_total * ri, width), lambda g, c: (0, 0)),
            pl.BlockSpec((chunk * ri, flat), lambda g, c: (g, 0)),
        ],
        out_specs=pl.BlockSpec((1, ri, chunk * ri), lambda g, c: (g, 0, 0)),
        scratch_shapes=[
            pltpu.VMEM((codes_total * ri, width), jnp.bfloat16),
            pltpu.VMEM((codes_total * ri, width), jnp.bfloat16),
            pltpu.VMEM((codes_total * ri, chunk * ri), jnp.float32),
        ],
    )
    body = lambda *refs: contract_kernel(*refs, slots=slots, width=width, ri=ri, chunk=chunk)
    out = pl.pallas_call(
        body, out_shape=jax.ShapeDtypeStruct((steps, ri, chunk * ri), jnp.float32), grid_spec=grid_spec
    )(codes, table2, xrows)
    return jnp.transpose(out, (1, 0, 2)).reshape(ri, groups * ri)


def on_device(x_blocks, pair_ids, live_count, green_occ, green_virt):
    local_blocks = x_blocks[0]
    slot_count, block_size, ri_cols = local_blocks.shape
    ri_local = ri_cols // block_size
    orbitals = green_occ.shape[0]
    band_orbs = 2 * block_size
    band_count = lax.axis_size("band")
    group_count = lax.axis_size("grp")
    band = lax.axis_index("band")
    flat = slot_count * block_size * block_size
    code_count = 2 * (orbitals // block_size)

    pair_list = pair_ids[0, 0]
    live_slots = live_count[0, 0]

    live = (jnp.arange(slot_count, dtype=jnp.int32) < live_slots).astype(local_blocks.dtype)
    masked = local_blocks * live[:, None, None]
    xt = masked.reshape(slot_count, block_size, ri_local, block_size)
    xt = jnp.transpose(xt, (2, 0, 3, 1)).reshape(ri_local, flat)
    meta = jnp.zeros((ri_local, META), local_blocks.dtype)
    meta = meta.at[0, :slot_count].set(pair_list.astype(local_blocks.dtype))
    packed = jnp.concatenate([xt, meta], axis=1)

    rows2d = masked.reshape(slot_count, block_size, ri_local, block_size)
    rows2d = jnp.transpose(rows2d, (0, 1, 3, 2)).reshape(slot_count * block_size, ri_cols)
    meta_rows = jnp.zeros((16, ri_cols), local_blocks.dtype)
    meta_rows = meta_rows.at[0, :slot_count].set(pair_list.astype(local_blocks.dtype))
    band_packed = jnp.concatenate([rows2d, meta_rows], axis=0)
    band_ids, band_got = ring_gather(band_packed, "band", band_count)
    xg = jnp.stack(band_got)
    kdim = slot_count * block_size
    codes_g = xg[:, kdim, :slot_count].astype(jnp.float32).astype(jnp.int32)
    grp_ids, grp_got = ring_gather(packed, "grp", group_count)
    xg, *early = lax.optimization_barrier([xg] + grp_got[3:5])
    grp_got[3:5] = early

    occ_cols = lax.dynamic_slice_in_dim(green_occ, band * band_orbs, band_orbs, 1)
    row_index = (codes_g // 2)[..., None] * block_size + jnp.arange(block_size, dtype=jnp.int32)
    occ_rows = jnp.take(occ_cols, row_index.reshape(-1), axis=0)
    occ_rows = occ_rows.reshape(band_count, slot_count, block_size, band_orbs)
    halves = (codes_g % 2)[:, None, :] == jnp.arange(2, dtype=jnp.int32)[None, :, None]
    occ_sel = occ_rows[:, None] * halves.astype(occ_rows.dtype)[..., None, None]
    occ_sel = occ_sel.reshape(band_count, 2, kdim, band_orbs)
    occ_raw = jnp.einsum(
        "bkr,bhkl->bhrl", xg[:, :kdim, :], occ_sel, preferred_element_type=jnp.float32
    ).astype(jnp.bfloat16)
    occ_raw = occ_raw.reshape(band_count, 2, block_size, ri_local, band_orbs)
    occ_raw, *later = lax.optimization_barrier([occ_raw] + grp_got[5:7])
    grp_got[5:7] = later

    virt_cols = jnp.concatenate(
        [lax.dynamic_slice_in_dim(green_virt, band_ids[k] * band_orbs, band_orbs, 1) for k in range(band_count)],
        axis=1,
    ).reshape(orbitals, band_count, 2, block_size)
    folded = lax.dot_general(
        occ_raw, virt_cols, (((0, 1, 2), (1, 2, 3)), ((), ())), preferred_element_type=jnp.float32
    )
    folded = lax.optimization_barrier(folded)
    folded = folded.reshape(ri_local, 2, block_size, orbitals // block_size, block_size)
    folded = jnp.transpose(folded, (3, 1, 0, 2, 4)).reshape(code_count, ri_local, block_size * block_size)
    xstack = jnp.stack(grp_got)
    codes_b = xstack[:, 0, flat:flat + slot_count].astype(jnp.float32).astype(jnp.int32)
    xrows = xstack.reshape(group_count * ri_local, flat + META)
    arrived = contract(codes_b, folded, xrows, group_count, slot_count, block_size * block_size)
    order = jnp.zeros((group_count,), jnp.int32).at[grp_ids].set(jnp.arange(group_count, dtype=jnp.int32))
    arrived = arrived.reshape(ri_local, group_count, ri_local)
    partial_value = jnp.take(arrived, order, axis=1).reshape(ri_local, group_count * ri_local)
    response = lax.psum_scatter(partial_value, "band", scatter_dimension=0, tiled=True)
    return response


def solution(mesh):
    placed = (P("band", None, None, "grp"), P("grp", "band", None), P("grp", "band"), P(), P())
    return jax.shard_map(
        on_device, mesh=mesh, in_specs=placed, out_specs=P(("grp", "band"), None), check_vma=False
    )
```

```python
import jax
import jax.numpy as jnp
from jax import lax
from jax.experimental import pallas as pl
from jax.experimental.pallas import tpu as pltpu
from jax.sharding import PartitionSpec as P

META = 128


def snake(count):
    half = count // 2
    return [2 * o for o in range(half)] + [2 * o + 1 for o in reversed(range(half))]


def ring_gather(buf, axis, count):
    order = snake(count)
    pos_of = [order.index(d) for d in range(count)]
    fwd = [(order[k], order[(k + 1) % count]) for k in range(count)]
    bwd = [(order[k], order[(k - 1) % count]) for k in range(count)]
    me = lax.axis_index(axis)
    pos = jnp.array(pos_of, jnp.int32)[me]
    order_arr = jnp.array(order, jnp.int32)
    shifts = [0]
    got = [buf]
    ahead = behind = buf
    for step in range(1, count // 2):
        ahead = lax.ppermute(ahead, axis, fwd)
        behind = lax.ppermute(behind, axis, bwd)
        got += [ahead, behind]
        shifts += [-step, step]
    rows = buf.shape[0] // 2
    first = lax.ppermute(ahead[:rows], axis, fwd)
    second = lax.ppermute(behind[rows:], axis, bwd)
    got.append(jnp.concatenate([first, second], axis=0))
    shifts.append(count // 2)
    sources = order_arr[(pos + jnp.array(shifts, jnp.int32)) % count]
    return sources, got


def contract_kernel(codes_ref, table_ref, x_ref, out_ref, hi_ref, lo_ref, dense_ref, *, slots, width, ri, chunk, blk):
    step = pl.program_id(0)

    @pl.when(step == 0)
    def split():
        lam_count = 2 * blk
        tiles = table_ref.shape[0] // (ri * lam_count)
        per_tile = 128 // blk
        for h in range(2):
            for j in range(blk):
                for t in range(tiles):
                    start = (h * blk + j) * tiles + t
                    rows = table_ref[pl.ds(start, ri, stride=lam_count * tiles), :]
                    hi = rows.astype(jnp.bfloat16)
                    lo = (rows - hi.astype(jnp.float32)).astype(jnp.bfloat16)
                    for u in range(per_tile):
                        code = 2 * (t * per_tile + u) + h
                        hi_ref[code * ri:(code + 1) * ri, j * blk:(j + 1) * blk] = hi[:, u * blk:(u + 1) * blk]
                        lo_ref[code * ri:(code + 1) * ri, j * blk:(j + 1) * blk] = lo[:, u * blk:(u + 1) * blk]

    out_ref[...] = jnp.zeros(out_ref.shape, jnp.float32)
    for s in range(slots):
        xs = x_ref[:, s * width:(s + 1) * width]
        dense = lax.dot_general(
            hi_ref[...], xs, (((1,), (1,)), ((), ())), preferred_element_type=jnp.float32
        )
        dense = dense + lax.dot_general(
            lo_ref[...], xs, (((1,), (1,)), ((), ())), preferred_element_type=jnp.float32
        )
        dense_ref[...] = dense
        for c in range(chunk):
            code = codes_ref[step * chunk + c, s]
            start = pl.multiple_of(code * ri, ri)
            out_ref[0, :, c * ri:(c + 1) * ri] += dense_ref[pl.ds(start, ri), c * ri:(c + 1) * ri]


def contract(codes, folded, xrows, groups, slots, blk):
    ri, lam_count, orbitals = folded.shape
    width = blk * blk
    codes_total = 2 * (orbitals // blk)
    flat = slots * width
    chunk = groups
    while chunk > 1 and (chunk * ri * flat * 2 > (4 << 20) or groups % chunk):
        chunk -= 1
    steps = groups // chunk
    table2 = folded.reshape(ri * lam_count * (orbitals // 128), 128)
    grid_spec = pltpu.PrefetchScalarGridSpec(
        num_scalar_prefetch=1,
        grid=(steps,),
        in_specs=[
            pl.BlockSpec(table2.shape, lambda g, c: (0, 0)),
            pl.BlockSpec((chunk * ri, flat), lambda g, c: (g, 0)),
        ],
        out_specs=pl.BlockSpec((1, ri, chunk * ri), lambda g, c: (g, 0, 0)),
        scratch_shapes=[
            pltpu.VMEM((codes_total * ri, width), jnp.bfloat16),
            pltpu.VMEM((codes_total * ri, width), jnp.bfloat16),
            pltpu.VMEM((codes_total * ri, chunk * ri), jnp.float32),
        ],
    )
    body = lambda *refs: contract_kernel(*refs, slots=slots, width=width, ri=ri, chunk=chunk, blk=blk)
    out = pl.pallas_call(
        body, out_shape=jax.ShapeDtypeStruct((steps, ri, chunk * ri), jnp.float32), grid_spec=grid_spec
    )(codes, table2, xrows)
    return jnp.transpose(out, (1, 0, 2)).reshape(ri, groups * ri)


def on_device(x_blocks, pair_ids, live_count, green_occ, green_virt):
    local_blocks = x_blocks[0]
    slot_count, block_size, ri_cols = local_blocks.shape
    ri_local = ri_cols // block_size
    orbitals = green_occ.shape[0]
    band_orbs = 2 * block_size
    band_count = lax.axis_size("band")
    group_count = lax.axis_size("grp")
    band = lax.axis_index("band")
    flat = slot_count * block_size * block_size
    code_count = 2 * (orbitals // block_size)

    pair_list = pair_ids[0, 0]
    live_slots = live_count[0, 0]

    live = (jnp.arange(slot_count, dtype=jnp.int32) < live_slots).astype(local_blocks.dtype)
    masked = local_blocks * live[:, None, None]
    xt = masked.reshape(slot_count, block_size, ri_local, block_size)
    xt = jnp.transpose(xt, (2, 0, 3, 1)).reshape(ri_local, flat)
    meta = jnp.zeros((ri_local, META), local_blocks.dtype)
    meta = meta.at[0, :slot_count].set(pair_list.astype(local_blocks.dtype))
    packed = jnp.concatenate([xt, meta], axis=1)

    rows2d = masked.reshape(slot_count, block_size, ri_local, block_size)
    rows2d = jnp.transpose(rows2d, (0, 1, 3, 2)).reshape(slot_count * block_size, ri_cols)
    meta_rows = jnp.zeros((16, ri_cols), local_blocks.dtype)
    meta_rows = meta_rows.at[0, :slot_count].set(pair_list.astype(local_blocks.dtype))
    band_packed = jnp.concatenate([rows2d, meta_rows], axis=0)
    band_ids, band_got = ring_gather(band_packed, "band", band_count)
    xg = jnp.stack(band_got)
    kdim = slot_count * block_size
    codes_g = xg[:, kdim, :slot_count].astype(jnp.float32).astype(jnp.int32)
    grp_ids, grp_got = ring_gather(packed, "grp", group_count)
    xg, *early = lax.optimization_barrier([xg] + grp_got[3:5])
    grp_got[3:5] = early

    occ_cols = lax.dynamic_slice_in_dim(green_occ, band * band_orbs, band_orbs, 1)
    row_index = (codes_g // 2)[..., None] * block_size + jnp.arange(block_size, dtype=jnp.int32)
    occ_rows = jnp.take(occ_cols, row_index.reshape(-1), axis=0)
    occ_rows = occ_rows.reshape(band_count, slot_count, block_size, band_orbs)
    halves = (codes_g % 2)[:, None, :] == jnp.arange(2, dtype=jnp.int32)[None, :, None]
    occ_sel = occ_rows[:, None] * halves.astype(occ_rows.dtype)[..., None, None]
    occ_sel = occ_sel.reshape(band_count, 2, kdim, band_orbs)
    occ_raw = jnp.einsum(
        "bkr,bhkl->bhrl", xg[:, :kdim, :], occ_sel, preferred_element_type=jnp.float32
    ).astype(jnp.bfloat16)
    occ_raw = occ_raw.reshape(band_count, 2, block_size, ri_local, band_orbs)
    occ_raw, *later = lax.optimization_barrier([occ_raw] + grp_got[5:7])
    grp_got[5:7] = later

    virt_cols = jnp.concatenate(
        [lax.dynamic_slice_in_dim(green_virt, band_ids[k] * band_orbs, band_orbs, 1) for k in range(band_count)],
        axis=1,
    ).reshape(orbitals, band_count, 2, block_size)
    folded = lax.dot_general(
        occ_raw, virt_cols, (((0, 1, 2), (1, 2, 3)), ((), ())), preferred_element_type=jnp.float32
    )
    xstack = jnp.stack(grp_got)
    codes_b = xstack[:, 0, flat:flat + slot_count].astype(jnp.float32).astype(jnp.int32)
    xrows = xstack.reshape(group_count * ri_local, flat + META)
    arrived = contract(codes_b, folded, xrows, group_count, slot_count, block_size)
    order = jnp.zeros((group_count,), jnp.int32).at[grp_ids].set(jnp.arange(group_count, dtype=jnp.int32))
    arrived = arrived.reshape(ri_local, group_count, ri_local)
    partial_value = jnp.take(arrived, order, axis=1).reshape(ri_local, group_count * ri_local)
    response = lax.psum_scatter(partial_value, "band", scatter_dimension=0, tiled=True)
    return response


def solution(mesh):
    placed = (P("band", None, None, "grp"), P("grp", "band", None), P("grp", "band"), P(), P())
    return jax.shard_map(
        on_device, mesh=mesh, in_specs=placed, out_specs=P(("grp", "band"), None), check_vma=False
    )
```

```python
import jax
import jax.numpy as jnp
from jax import lax
from jax.experimental import pallas as pl
from jax.experimental.pallas import tpu as pltpu
from jax.sharding import PartitionSpec as P

META = 128


def snake(count):
    half = count // 2
    return [2 * o for o in range(half)] + [2 * o + 1 for o in reversed(range(half))]


def ring_gather(buf, axis, count):
    order = snake(count)
    pos_of = [order.index(d) for d in range(count)]
    fwd = [(order[k], order[(k + 1) % count]) for k in range(count)]
    bwd = [(order[k], order[(k - 1) % count]) for k in range(count)]
    me = lax.axis_index(axis)
    pos = jnp.array(pos_of, jnp.int32)[me]
    order_arr = jnp.array(order, jnp.int32)
    shifts = [0]
    got = [buf]
    ahead = behind = buf
    for step in range(1, count // 2):
        ahead = lax.ppermute(ahead, axis, fwd)
        behind = lax.ppermute(behind, axis, bwd)
        got += [ahead, behind]
        shifts += [-step, step]
    rows = buf.shape[0] // 2
    first = lax.ppermute(ahead[:rows], axis, fwd)
    second = lax.ppermute(behind[rows:], axis, bwd)
    got.append(jnp.concatenate([first, second], axis=0))
    shifts.append(count // 2)
    sources = order_arr[(pos + jnp.array(shifts, jnp.int32)) % count]
    return sources, got


def contract_kernel(codes_ref, table_ref, x_ref, out_ref, hi_ref, lo_ref, dense_ref, *, slots, width, ri, chunk, blk):
    step = pl.program_id(0)

    @pl.when(step == 0)
    def split():
        lam_count = 2 * blk
        tiles = table_ref.shape[0] // (ri * lam_count)
        per_tile = 128 // blk
        for h in range(2):
            for j in range(blk):
                for t in range(tiles):
                    lam = h * blk + j
                    start = ((lam // 8) * tiles + t) * 8 + lam % 8
                    rows = table_ref[pl.ds(start, ri, stride=lam_count * tiles), :]
                    hi = rows.astype(jnp.bfloat16)
                    lo = (rows - hi.astype(jnp.float32)).astype(jnp.bfloat16)
                    for u in range(per_tile):
                        code = 2 * (t * per_tile + u) + h
                        hi_ref[code * ri:(code + 1) * ri, j * blk:(j + 1) * blk] = hi[:, u * blk:(u + 1) * blk]
                        lo_ref[code * ri:(code + 1) * ri, j * blk:(j + 1) * blk] = lo[:, u * blk:(u + 1) * blk]

    out_ref[...] = jnp.zeros(out_ref.shape, jnp.float32)
    for s in range(slots):
        xs = x_ref[:, s * width:(s + 1) * width]
        dense = lax.dot_general(
            hi_ref[...], xs, (((1,), (1,)), ((), ())), preferred_element_type=jnp.float32
        )
        dense = dense + lax.dot_general(
            lo_ref[...], xs, (((1,), (1,)), ((), ())), preferred_element_type=jnp.float32
        )
        dense_ref[...] = dense
        for c in range(chunk):
            code = codes_ref[step * chunk + c, s]
            start = pl.multiple_of(code * ri, ri)
            out_ref[0, :, c * ri:(c + 1) * ri] += dense_ref[pl.ds(start, ri), c * ri:(c + 1) * ri]


def contract(codes, folded, xrows, groups, slots, blk):
    ri, lam_count, orbitals = folded.shape
    width = blk * blk
    codes_total = 2 * (orbitals // blk)
    flat = slots * width
    chunk = groups
    while chunk > 1 and (chunk * ri * flat * 2 > (4 << 20) or groups % chunk):
        chunk -= 1
    steps = groups // chunk
    tiles = orbitals // 128
    table2 = folded.reshape(ri, lam_count // 8, 8, tiles, 128)
    table2 = jnp.transpose(table2, (0, 1, 3, 2, 4)).reshape(ri * lam_count * tiles, 128)
    grid_spec = pltpu.PrefetchScalarGridSpec(
        num_scalar_prefetch=1,
        grid=(steps,),
        in_specs=[
            pl.BlockSpec(table2.shape, lambda g, c: (0, 0)),
            pl.BlockSpec((chunk * ri, flat), lambda g, c: (g, 0)),
        ],
        out_specs=pl.BlockSpec((1, ri, chunk * ri), lambda g, c: (g, 0, 0)),
        scratch_shapes=[
            pltpu.VMEM((codes_total * ri, width), jnp.bfloat16),
            pltpu.VMEM((codes_total * ri, width), jnp.bfloat16),
            pltpu.VMEM((codes_total * ri, chunk * ri), jnp.float32),
        ],
    )
    body = lambda *refs: contract_kernel(*refs, slots=slots, width=width, ri=ri, chunk=chunk, blk=blk)
    out = pl.pallas_call(
        body, out_shape=jax.ShapeDtypeStruct((steps, ri, chunk * ri), jnp.float32), grid_spec=grid_spec
    )(codes, table2, xrows)
    return jnp.transpose(out, (1, 0, 2)).reshape(ri, groups * ri)


def on_device(x_blocks, pair_ids, live_count, green_occ, green_virt):
    local_blocks = x_blocks[0]
    slot_count, block_size, ri_cols = local_blocks.shape
    ri_local = ri_cols // block_size
    orbitals = green_occ.shape[0]
    band_orbs = 2 * block_size
    band_count = lax.axis_size("band")
    group_count = lax.axis_size("grp")
    band = lax.axis_index("band")
    flat = slot_count * block_size * block_size
    code_count = 2 * (orbitals // block_size)

    pair_list = pair_ids[0, 0]
    live_slots = live_count[0, 0]

    live = (jnp.arange(slot_count, dtype=jnp.int32) < live_slots).astype(local_blocks.dtype)
    masked = local_blocks * live[:, None, None]
    xt = masked.reshape(slot_count, block_size, ri_local, block_size)
    xt = jnp.transpose(xt, (2, 0, 3, 1)).reshape(ri_local, flat)
    meta = jnp.zeros((ri_local, META), local_blocks.dtype)
    meta = meta.at[0, :slot_count].set(pair_list.astype(local_blocks.dtype))
    packed = jnp.concatenate([xt, meta], axis=1)

    rows2d = masked.reshape(slot_count, block_size, ri_local, block_size)
    rows2d = jnp.transpose(rows2d, (0, 1, 3, 2)).reshape(slot_count * block_size, ri_cols)
    meta_rows = jnp.zeros((16, ri_cols), local_blocks.dtype)
    meta_rows = meta_rows.at[0, :slot_count].set(pair_list.astype(local_blocks.dtype))
    band_packed = jnp.concatenate([rows2d, meta_rows], axis=0)
    band_ids, band_got = ring_gather(band_packed, "band", band_count)
    xg = jnp.stack(band_got)
    kdim = slot_count * block_size
    codes_g = xg[:, kdim, :slot_count].astype(jnp.float32).astype(jnp.int32)
    grp_ids, grp_got = ring_gather(packed, "grp", group_count)
    xg, *early = lax.optimization_barrier([xg] + grp_got[3:5])
    grp_got[3:5] = early

    occ_cols = lax.dynamic_slice_in_dim(green_occ, band * band_orbs, band_orbs, 1)
    row_index = (codes_g // 2)[..., None] * block_size + jnp.arange(block_size, dtype=jnp.int32)
    occ_rows = jnp.take(occ_cols, row_index.reshape(-1), axis=0)
    occ_rows = occ_rows.reshape(band_count, slot_count, block_size, band_orbs)
    halves = (codes_g % 2)[:, None, :] == jnp.arange(2, dtype=jnp.int32)[None, :, None]
    occ_sel = occ_rows[:, None] * halves.astype(occ_rows.dtype)[..., None, None]
    occ_sel = occ_sel.reshape(band_count, 2, kdim, band_orbs)
    occ_raw = jnp.einsum(
        "bkr,bhkl->bhrl", xg[:, :kdim, :], occ_sel, preferred_element_type=jnp.float32
    ).astype(jnp.bfloat16)
    occ_raw = occ_raw.reshape(band_count, 2, block_size, ri_local, band_orbs)
    occ_raw, *later = lax.optimization_barrier([occ_raw] + grp_got[5:7])
    grp_got[5:7] = later

    virt_cols = jnp.concatenate(
        [lax.dynamic_slice_in_dim(green_virt, band_ids[k] * band_orbs, band_orbs, 1) for k in range(band_count)],
        axis=1,
    ).reshape(orbitals, band_count, 2, block_size)
    folded = lax.dot_general(
        occ_raw, virt_cols, (((0, 1, 2), (1, 2, 3)), ((), ())), preferred_element_type=jnp.float32
    )
    xstack = jnp.stack(grp_got)
    codes_b = xstack[:, 0, flat:flat + slot_count].astype(jnp.float32).astype(jnp.int32)
    xrows = xstack.reshape(group_count * ri_local, flat + META)
    arrived = contract(codes_b, folded, xrows, group_count, slot_count, block_size)
    order = jnp.zeros((group_count,), jnp.int32).at[grp_ids].set(jnp.arange(group_count, dtype=jnp.int32))
    arrived = arrived.reshape(ri_local, group_count, ri_local)
    partial_value = jnp.take(arrived, order, axis=1).reshape(ri_local, group_count * ri_local)
    response = lax.psum_scatter(partial_value, "band", scatter_dimension=0, tiled=True)
    return response


def solution(mesh):
    placed = (P("band", None, None, "grp"), P("grp", "band", None), P("grp", "band"), P(), P())
    return jax.shard_map(
        on_device, mesh=mesh, in_specs=placed, out_specs=P(("grp", "band"), None), check_vma=False
    )
```

```python
import jax
import jax.numpy as jnp
from jax import lax
from jax.experimental import pallas as pl
from jax.experimental.pallas import tpu as pltpu
from jax.sharding import PartitionSpec as P

META = 128


def snake(count):
    half = count // 2
    return [2 * o for o in range(half)] + [2 * o + 1 for o in reversed(range(half))]


def ring_gather(buf, axis, count):
    order = snake(count)
    pos_of = [order.index(d) for d in range(count)]
    fwd = [(order[k], order[(k + 1) % count]) for k in range(count)]
    bwd = [(order[k], order[(k - 1) % count]) for k in range(count)]
    me = lax.axis_index(axis)
    pos = jnp.array(pos_of, jnp.int32)[me]
    order_arr = jnp.array(order, jnp.int32)
    shifts = [0]
    got = [buf]
    ahead = behind = buf
    for step in range(1, count // 2):
        ahead = lax.ppermute(ahead, axis, fwd)
        behind = lax.ppermute(behind, axis, bwd)
        got += [ahead, behind]
        shifts += [-step, step]
    rows = buf.shape[0] // 2
    first = lax.ppermute(ahead[:rows], axis, fwd)
    second = lax.ppermute(behind[rows:], axis, bwd)
    got.append(jnp.concatenate([first, second], axis=0))
    shifts.append(count // 2)
    sources = order_arr[(pos + jnp.array(shifts, jnp.int32)) % count]
    return sources, got


def contract_kernel(codes_ref, table_ref, x_ref, out_ref, hi_ref, lo_ref, dense_ref, *, slots, width, ri, chunk, blk):
    step = pl.program_id(0)

    @pl.when(step == 0)
    def split():
        lam_count = 2 * blk
        tiles = table_ref.shape[0] // (ri * lam_count)
        per_tile = 128 // blk
        for h in range(2):
            for j in range(blk):
                for t in range(tiles):
                    lam = h * blk + j
                    start = ((lam // 8) * tiles + t) * 8 + lam % 8
                    rows = table_ref[pl.ds(start, ri, stride=lam_count * tiles), :]
                    hi = rows.astype(jnp.bfloat16)
                    lo = (rows - hi.astype(jnp.float32)).astype(jnp.bfloat16)
                    for u in range(per_tile):
                        code = 2 * (t * per_tile + u) + h
                        hi_ref[code * ri:(code + 1) * ri, j * blk:(j + 1) * blk] = hi[:, u * blk:(u + 1) * blk]
                        lo_ref[code * ri:(code + 1) * ri, j * blk:(j + 1) * blk] = lo[:, u * blk:(u + 1) * blk]

    out_ref[...] = jnp.zeros(out_ref.shape, jnp.float32)
    for s in range(slots):
        xs = x_ref[:, s * width:(s + 1) * width]
        dense = lax.dot_general(
            hi_ref[...], xs, (((1,), (1,)), ((), ())), preferred_element_type=jnp.float32
        )
        dense = dense + lax.dot_general(
            lo_ref[...], xs, (((1,), (1,)), ((), ())), preferred_element_type=jnp.float32
        )
        dense_ref[...] = dense
        for c in range(chunk):
            code = codes_ref[step * chunk + c, s]
            start = pl.multiple_of(code * ri, ri)
            out_ref[0, :, c * ri:(c + 1) * ri] += dense_ref[pl.ds(start, ri), c * ri:(c + 1) * ri]


def contract(codes, folded, xrows, groups, slots, blk):
    ri, lam_count, orbitals = folded.shape
    width = blk * blk
    codes_total = 2 * (orbitals // blk)
    flat = slots * width
    chunk = groups
    while chunk > 1 and (chunk * ri * flat * 2 > (4 << 20) or groups % chunk):
        chunk -= 1
    steps = groups // chunk
    tiles = orbitals // 128
    table2 = folded.reshape(ri, lam_count // 8, 8, tiles, 128)
    table2 = jnp.transpose(table2, (0, 1, 3, 2, 4)).reshape(ri * lam_count * tiles, 128)
    grid_spec = pltpu.PrefetchScalarGridSpec(
        num_scalar_prefetch=1,
        grid=(steps,),
        in_specs=[
            pl.BlockSpec(table2.shape, lambda g, c: (0, 0)),
            pl.BlockSpec((chunk * ri, flat), lambda g, c: (g, 0)),
        ],
        out_specs=pl.BlockSpec((1, ri, chunk * ri), lambda g, c: (g, 0, 0)),
        scratch_shapes=[
            pltpu.VMEM((codes_total * ri, width), jnp.bfloat16),
            pltpu.VMEM((codes_total * ri, width), jnp.bfloat16),
            pltpu.VMEM((codes_total * ri, chunk * ri), jnp.float32),
        ],
    )
    body = lambda *refs: contract_kernel(*refs, slots=slots, width=width, ri=ri, chunk=chunk, blk=blk)
    out = pl.pallas_call(
        body, out_shape=jax.ShapeDtypeStruct((steps, ri, chunk * ri), jnp.float32), grid_spec=grid_spec
    )(codes, table2, xrows)
    return jnp.transpose(out, (1, 0, 2)).reshape(ri, groups * ri)


def on_device(x_blocks, pair_ids, live_count, green_occ, green_virt):
    local_blocks = x_blocks[0]
    slot_count, block_size, ri_cols = local_blocks.shape
    ri_local = ri_cols // block_size
    orbitals = green_occ.shape[0]
    band_orbs = 2 * block_size
    band_count = lax.axis_size("band")
    group_count = lax.axis_size("grp")
    band = lax.axis_index("band")
    flat = slot_count * block_size * block_size
    code_count = 2 * (orbitals // block_size)

    pair_list = pair_ids[0, 0]
    live_slots = live_count[0, 0]

    live = (jnp.arange(slot_count, dtype=jnp.int32) < live_slots).astype(local_blocks.dtype)
    masked = local_blocks * live[:, None, None]
    xt = masked.reshape(slot_count, block_size, ri_local, block_size)
    xt = jnp.transpose(xt, (2, 0, 3, 1)).reshape(ri_local, flat)
    meta = jnp.zeros((ri_local, META), local_blocks.dtype)
    meta = meta.at[0, :slot_count].set(pair_list.astype(local_blocks.dtype))
    packed = jnp.concatenate([xt, meta], axis=1)

    rows2d = masked.reshape(slot_count, block_size, ri_local, block_size)
    rows2d = jnp.transpose(rows2d, (0, 1, 3, 2)).reshape(slot_count * block_size, ri_cols)
    meta_rows = jnp.zeros((16, ri_cols), local_blocks.dtype)
    meta_rows = meta_rows.at[0, :slot_count].set(pair_list.astype(local_blocks.dtype))
    band_packed = jnp.concatenate([rows2d, meta_rows], axis=0)
    band_ids, band_got = ring_gather(band_packed, "band", band_count)
    xg = jnp.stack(band_got)
    kdim = slot_count * block_size
    codes_g = xg[:, kdim, :slot_count].astype(jnp.float32).astype(jnp.int32)
    grp_ids, grp_got = ring_gather(packed, "grp", group_count)
    xg, *early = lax.optimization_barrier([xg] + grp_got[3:5])
    grp_got[3:5] = early

    occ_cols = lax.dynamic_slice_in_dim(green_occ, band * band_orbs, band_orbs, 1)
    row_index = (codes_g // 2)[..., None] * block_size + jnp.arange(block_size, dtype=jnp.int32)
    occ_rows = jnp.take(occ_cols, row_index.reshape(-1), axis=0)
    occ_rows = occ_rows.reshape(band_count, slot_count, block_size, band_orbs)
    halves = (codes_g % 2)[:, None, :] == jnp.arange(2, dtype=jnp.int32)[None, :, None]
    occ_sel = occ_rows[:, None] * halves.astype(occ_rows.dtype)[..., None, None]
    occ_sel = occ_sel.reshape(band_count, 2, kdim, band_orbs)
    occ_raw = jnp.einsum(
        "bkr,bhkl->bhrl", xg[:, :kdim, :], occ_sel, preferred_element_type=jnp.float32
    ).astype(jnp.bfloat16)
    occ_raw = occ_raw.reshape(band_count, 2, block_size, ri_local, band_orbs)
    occ_raw, *later = lax.optimization_barrier([occ_raw] + grp_got[5:7])
    grp_got[5:7] = later

    virt_cols = jnp.concatenate(
        [lax.dynamic_slice_in_dim(green_virt, band_ids[k] * band_orbs, band_orbs, 1) for k in range(band_count)],
        axis=1,
    ).reshape(orbitals, band_count, 2, block_size)
    folded = lax.dot_general(
        occ_raw, virt_cols, (((0, 1, 2), (1, 2, 3)), ((), ())), preferred_element_type=jnp.float32
    )
    xstack = jnp.stack(grp_got)
    codes_b = xstack[:, 0, flat:flat + slot_count].astype(jnp.float32).astype(jnp.int32)
    xrows = xstack.reshape(group_count * ri_local, flat + META)
    arrived = contract(codes_b, folded, xrows, group_count, slot_count, block_size)
    order = jnp.zeros((group_count,), jnp.int32).at[grp_ids].set(jnp.arange(group_count, dtype=jnp.int32))
    arrived = arrived.reshape(ri_local, group_count, ri_local)
    partial_value = jnp.take(arrived, order, axis=1).reshape(ri_local, group_count * ri_local)
    rows_out = ri_local // band_count
    blocks = partial_value.reshape(band_count, rows_out, group_count * ri_local)
    response = lax.dynamic_index_in_dim(blocks, band, 0, keepdims=False)
    for shift in range(1, band_count):
        sent = lax.dynamic_index_in_dim(blocks, (band + shift) % band_count, 0, keepdims=False)
        pairs = [(i, (i + shift) % band_count) for i in range(band_count)]
        response = response + lax.ppermute(sent, "band", pairs)
    return response


def solution(mesh):
    placed = (P("band", None, None, "grp"), P("grp", "band", None), P("grp", "band"), P(), P())
    return jax.shard_map(
        on_device, mesh=mesh, in_specs=placed, out_specs=P(("grp", "band"), None), check_vma=False
    )
```

```python
import jax
import jax.numpy as jnp
from jax import lax
from jax.experimental import pallas as pl
from jax.experimental.pallas import tpu as pltpu
from jax.sharding import PartitionSpec as P

META = 128


def snake(count):
    half = count // 2
    return [2 * o for o in range(half)] + [2 * o + 1 for o in reversed(range(half))]


def ring_gather(buf, axis, count):
    order = snake(count)
    pos_of = [order.index(d) for d in range(count)]
    fwd = [(order[k], order[(k + 1) % count]) for k in range(count)]
    bwd = [(order[k], order[(k - 1) % count]) for k in range(count)]
    me = lax.axis_index(axis)
    pos = jnp.array(pos_of, jnp.int32)[me]
    order_arr = jnp.array(order, jnp.int32)
    shifts = [0]
    got = [buf]
    ahead = behind = buf
    for step in range(1, count // 2):
        ahead = lax.ppermute(ahead, axis, fwd)
        behind = lax.ppermute(behind, axis, bwd)
        got += [ahead, behind]
        shifts += [-step, step]
    rows = buf.shape[0] // 2
    first = lax.ppermute(ahead[:rows], axis, fwd)
    second = lax.ppermute(behind[rows:], axis, bwd)
    got.append(jnp.concatenate([first, second], axis=0))
    shifts.append(count // 2)
    sources = order_arr[(pos + jnp.array(shifts, jnp.int32)) % count]
    return sources, got


def contract_kernel(codes_ref, table_ref, x_ref, out_ref, both_ref, dense_ref, *, slots, width, ri, chunk, blk):
    step = pl.program_id(0)

    @pl.when(step == 0)
    def split():
        lam_count = 2 * blk
        half = both_ref.shape[0] // (2 * ri)
        tiles = table_ref.shape[0] // (ri * lam_count)
        per_tile = 128 // blk
        for h in range(2):
            for j in range(blk):
                for t in range(tiles):
                    lam = h * blk + j
                    start = ((lam // 8) * tiles + t) * 8 + lam % 8
                    rows = table_ref[pl.ds(start, ri, stride=lam_count * tiles), :]
                    hi = rows.astype(jnp.bfloat16)
                    lo = (rows - hi.astype(jnp.float32)).astype(jnp.bfloat16)
                    for u in range(per_tile):
                        code = 2 * (t * per_tile + u) + h
                        both_ref[code * ri:(code + 1) * ri, j * blk:(j + 1) * blk] = hi[:, u * blk:(u + 1) * blk]
                        low = (half + code) * ri
                        both_ref[low:low + ri, j * blk:(j + 1) * blk] = lo[:, u * blk:(u + 1) * blk]

    out_ref[...] = jnp.zeros(out_ref.shape, jnp.float32)
    for s in range(slots):
        xs = x_ref[:, s * width:(s + 1) * width]
        dense = lax.dot_general(
            both_ref[...], xs, (((1,), (1,)), ((), ())), preferred_element_type=jnp.float32
        )
        dense_ref[...] = dense
        for c in range(chunk):
            code = codes_ref[step * chunk + c, s]
            start = pl.multiple_of(code * ri, ri)
            low = pl.multiple_of((code + dense_ref.shape[0] // (2 * ri)) * ri, ri)
            out_ref[0, :, c * ri:(c + 1) * ri] += (
                dense_ref[pl.ds(start, ri), c * ri:(c + 1) * ri] + dense_ref[pl.ds(low, ri), c * ri:(c + 1) * ri]
            )


def contract(codes, folded, xrows, groups, slots, blk):
    ri, lam_count, orbitals = folded.shape
    width = blk * blk
    codes_total = 2 * (orbitals // blk)
    flat = slots * width
    chunk = groups
    while chunk > 1 and (chunk * ri * flat * 2 > (4 << 20) or groups % chunk):
        chunk -= 1
    steps = groups // chunk
    tiles = orbitals // 128
    table2 = folded.reshape(ri, lam_count // 8, 8, tiles, 128)
    table2 = jnp.transpose(table2, (0, 1, 3, 2, 4)).reshape(ri * lam_count * tiles, 128)
    grid_spec = pltpu.PrefetchScalarGridSpec(
        num_scalar_prefetch=1,
        grid=(steps,),
        in_specs=[
            pl.BlockSpec(table2.shape, lambda g, c: (0, 0)),
            pl.BlockSpec((chunk * ri, flat), lambda g, c: (g, 0)),
        ],
        out_specs=pl.BlockSpec((1, ri, chunk * ri), lambda g, c: (g, 0, 0)),
        scratch_shapes=[
            pltpu.VMEM((2 * codes_total * ri, width), jnp.bfloat16),
            pltpu.VMEM((2 * codes_total * ri, chunk * ri), jnp.float32),
        ],
    )
    body = lambda *refs: contract_kernel(*refs, slots=slots, width=width, ri=ri, chunk=chunk, blk=blk)
    out = pl.pallas_call(
        body, out_shape=jax.ShapeDtypeStruct((steps, ri, chunk * ri), jnp.float32), grid_spec=grid_spec
    )(codes, table2, xrows)
    return jnp.transpose(out, (1, 0, 2)).reshape(ri, groups * ri)


def on_device(x_blocks, pair_ids, live_count, green_occ, green_virt):
    local_blocks = x_blocks[0]
    slot_count, block_size, ri_cols = local_blocks.shape
    ri_local = ri_cols // block_size
    orbitals = green_occ.shape[0]
    band_orbs = 2 * block_size
    band_count = lax.axis_size("band")
    group_count = lax.axis_size("grp")
    band = lax.axis_index("band")
    flat = slot_count * block_size * block_size
    code_count = 2 * (orbitals // block_size)

    pair_list = pair_ids[0, 0]
    live_slots = live_count[0, 0]

    live = (jnp.arange(slot_count, dtype=jnp.int32) < live_slots).astype(local_blocks.dtype)
    masked = local_blocks * live[:, None, None]
    xt = masked.reshape(slot_count, block_size, ri_local, block_size)
    xt = jnp.transpose(xt, (2, 0, 3, 1)).reshape(ri_local, flat)
    meta = jnp.zeros((ri_local, META), local_blocks.dtype)
    meta = meta.at[0, :slot_count].set(pair_list.astype(local_blocks.dtype))
    packed = jnp.concatenate([xt, meta], axis=1)

    rows2d = masked.reshape(slot_count, block_size, ri_local, block_size)
    rows2d = jnp.transpose(rows2d, (0, 1, 3, 2)).reshape(slot_count * block_size, ri_cols)
    meta_rows = jnp.zeros((16, ri_cols), local_blocks.dtype)
    meta_rows = meta_rows.at[0, :slot_count].set(pair_list.astype(local_blocks.dtype))
    band_packed = jnp.concatenate([rows2d, meta_rows], axis=0)
    band_ids, band_got = ring_gather(band_packed, "band", band_count)
    xg = jnp.stack(band_got)
    kdim = slot_count * block_size
    codes_g = xg[:, kdim, :slot_count].astype(jnp.float32).astype(jnp.int32)
    grp_ids, grp_got = ring_gather(packed, "grp", group_count)
    xg, *early = lax.optimization_barrier([xg] + grp_got[3:5])
    grp_got[3:5] = early

    occ_cols = lax.dynamic_slice_in_dim(green_occ, band * band_orbs, band_orbs, 1)
    row_index = (codes_g // 2)[..., None] * block_size + jnp.arange(block_size, dtype=jnp.int32)
    occ_rows = jnp.take(occ_cols, row_index.reshape(-1), axis=0)
    occ_rows = occ_rows.reshape(band_count, slot_count, block_size, band_orbs)
    halves = (codes_g % 2)[:, None, :] == jnp.arange(2, dtype=jnp.int32)[None, :, None]
    occ_sel = occ_rows[:, None] * halves.astype(occ_rows.dtype)[..., None, None]
    occ_sel = occ_sel.reshape(band_count, 2, kdim, band_orbs)
    occ_raw = jnp.einsum(
        "bkr,bhkl->bhrl", xg[:, :kdim, :], occ_sel, preferred_element_type=jnp.float32
    ).astype(jnp.bfloat16)
    occ_raw = occ_raw.reshape(band_count, 2, block_size, ri_local, band_orbs)
    occ_raw, *later = lax.optimization_barrier([occ_raw] + grp_got[5:7])
    grp_got[5:7] = later

    virt_cols = jnp.concatenate(
        [lax.dynamic_slice_in_dim(green_virt, band_ids[k] * band_orbs, band_orbs, 1) for k in range(band_count)],
        axis=1,
    ).reshape(orbitals, band_count, 2, block_size)
    folded = lax.dot_general(
        occ_raw, virt_cols, (((0, 1, 2), (1, 2, 3)), ((), ())), preferred_element_type=jnp.float32
    )
    xstack = jnp.stack(grp_got)
    codes_b = xstack[:, 0, flat:flat + slot_count].astype(jnp.float32).astype(jnp.int32)
    xrows = xstack.reshape(group_count * ri_local, flat + META)
    arrived = contract(codes_b, folded, xrows, group_count, slot_count, block_size)
    order = jnp.zeros((group_count,), jnp.int32).at[grp_ids].set(jnp.arange(group_count, dtype=jnp.int32))
    arrived = arrived.reshape(ri_local, group_count, ri_local)
    partial_value = jnp.take(arrived, order, axis=1).reshape(ri_local, group_count * ri_local)
    rows_out = ri_local // band_count
    blocks = partial_value.reshape(band_count, rows_out, group_count * ri_local)
    response = lax.dynamic_index_in_dim(blocks, band, 0, keepdims=False)
    for shift in range(1, band_count):
        sent = lax.dynamic_index_in_dim(blocks, (band + shift) % band_count, 0, keepdims=False)
        pairs = [(i, (i + shift) % band_count) for i in range(band_count)]
        response = response + lax.ppermute(sent, "band", pairs)
    return response


def solution(mesh):
    placed = (P("band", None, None, "grp"), P("grp", "band", None), P("grp", "band"), P(), P())
    return jax.shard_map(
        on_device, mesh=mesh, in_specs=placed, out_specs=P(("grp", "band"), None), check_vma=False
    )
```

```python
import jax
import jax.numpy as jnp
from jax import lax
from jax.experimental import pallas as pl
from jax.experimental.pallas import tpu as pltpu
from jax.sharding import PartitionSpec as P

META = 128


def snake(count):
    half = count // 2
    return [2 * o for o in range(half)] + [2 * o + 1 for o in reversed(range(half))]


def ring_gather(buf, axis, count):
    order = snake(count)
    pos_of = [order.index(d) for d in range(count)]
    fwd = [(order[k], order[(k + 1) % count]) for k in range(count)]
    bwd = [(order[k], order[(k - 1) % count]) for k in range(count)]
    me = lax.axis_index(axis)
    pos = jnp.array(pos_of, jnp.int32)[me]
    order_arr = jnp.array(order, jnp.int32)
    shifts = [0]
    got = [buf]
    ahead = behind = buf
    for step in range(1, count // 2):
        ahead = lax.ppermute(ahead, axis, fwd)
        behind = lax.ppermute(behind, axis, bwd)
        got += [ahead, behind]
        shifts += [-step, step]
    rows = buf.shape[0] // 2
    first = lax.ppermute(ahead[:rows], axis, fwd)
    second = lax.ppermute(behind[rows:], axis, bwd)
    got.append(jnp.concatenate([first, second], axis=0))
    shifts.append(count // 2)
    sources = order_arr[(pos + jnp.array(shifts, jnp.int32)) % count]
    return sources, got


def contract_kernel(codes_ref, table_ref, x_ref, out_ref, both_ref, dense_ref, *, slots, width, ri, chunk, blk):
    step = pl.program_id(0)

    @pl.when(step == 0)
    def split():
        lam_count = 2 * blk
        half = both_ref.shape[0] // (2 * ri)
        tiles = table_ref.shape[0] // (ri * lam_count)
        per_tile = 128 // blk
        for h in range(2):
            for j in range(blk):
                for t in range(tiles):
                    lam = h * blk + j
                    start = ((lam // 8) * tiles + t) * 8 + lam % 8
                    rows = table_ref[pl.ds(start, ri, stride=lam_count * tiles), :]
                    hi = rows.astype(jnp.bfloat16)
                    lo = (rows - hi.astype(jnp.float32)).astype(jnp.bfloat16)
                    for u in range(per_tile):
                        code = 2 * (t * per_tile + u) + h
                        both_ref[code * ri:(code + 1) * ri, j * blk:(j + 1) * blk] = hi[:, u * blk:(u + 1) * blk]
                        low = (half + code) * ri
                        both_ref[low:low + ri, j * blk:(j + 1) * blk] = lo[:, u * blk:(u + 1) * blk]

    out_ref[...] = jnp.zeros(out_ref.shape, jnp.float32)
    for s in range(slots):
        xs = x_ref[:, s * width:(s + 1) * width]
        dense = lax.dot_general(
            both_ref[...], xs, (((1,), (1,)), ((), ())), preferred_element_type=jnp.float32
        )
        dense_ref[...] = dense
        for c in range(chunk):
            code = codes_ref[step * chunk + c, s]
            start = pl.multiple_of(code * ri, ri)
            low = pl.multiple_of((code + dense_ref.shape[0] // (2 * ri)) * ri, ri)
            out_ref[0, :, c * ri:(c + 1) * ri] += (
                dense_ref[pl.ds(start, ri), c * ri:(c + 1) * ri] + dense_ref[pl.ds(low, ri), c * ri:(c + 1) * ri]
            )


def contract(codes, folded, xrows, groups, slots, blk):
    ri, lam_count, orbitals = folded.shape
    width = blk * blk
    codes_total = 2 * (orbitals // blk)
    flat = slots * width
    chunk = groups
    while chunk > 1 and (chunk * ri * flat * 2 > (4 << 20) or groups % chunk):
        chunk -= 1
    steps = groups // chunk
    tiles = orbitals // 128
    table2 = folded.reshape(ri, lam_count // 8, 8, tiles, 128)
    table2 = jnp.transpose(table2, (0, 1, 3, 2, 4)).reshape(ri * lam_count * tiles, 128)
    grid_spec = pltpu.PrefetchScalarGridSpec(
        num_scalar_prefetch=1,
        grid=(steps,),
        in_specs=[
            pl.BlockSpec(table2.shape, lambda g, c: (0, 0)),
            pl.BlockSpec((chunk * ri, flat), lambda g, c: (g, 0)),
        ],
        out_specs=pl.BlockSpec((1, ri, chunk * ri), lambda g, c: (g, 0, 0)),
        scratch_shapes=[
            pltpu.VMEM((2 * codes_total * ri, width), jnp.bfloat16),
            pltpu.VMEM((2 * codes_total * ri, chunk * ri), jnp.float32),
        ],
    )
    body = lambda *refs: contract_kernel(*refs, slots=slots, width=width, ri=ri, chunk=chunk, blk=blk)
    out = pl.pallas_call(
        body, out_shape=jax.ShapeDtypeStruct((steps, ri, chunk * ri), jnp.float32), grid_spec=grid_spec
    )(codes, table2, xrows)
    return jnp.transpose(out, (1, 0, 2)).reshape(ri, groups * ri)


def on_device(x_blocks, pair_ids, live_count, green_occ, green_virt):
    local_blocks = x_blocks[0]
    slot_count, block_size, ri_cols = local_blocks.shape
    ri_local = ri_cols // block_size
    orbitals = green_occ.shape[0]
    band_orbs = 2 * block_size
    band_count = lax.axis_size("band")
    group_count = lax.axis_size("grp")
    band = lax.axis_index("band")
    flat = slot_count * block_size * block_size
    code_count = 2 * (orbitals // block_size)

    pair_list = pair_ids[0, 0]
    live_slots = live_count[0, 0]

    live = (jnp.arange(slot_count, dtype=jnp.int32) < live_slots).astype(local_blocks.dtype)
    masked = local_blocks * live[:, None, None]
    xt = masked.reshape(slot_count, block_size, ri_local, block_size)
    xt = jnp.transpose(xt, (2, 0, 3, 1)).reshape(ri_local, flat)
    meta = jnp.zeros((ri_local, META), local_blocks.dtype)
    meta = meta.at[0, :slot_count].set(pair_list.astype(local_blocks.dtype))
    packed = jnp.concatenate([xt, meta], axis=1)

    rows2d = masked.reshape(slot_count, block_size, ri_local, block_size)
    rows2d = jnp.transpose(rows2d, (0, 1, 3, 2)).reshape(slot_count * block_size, ri_cols)
    meta_rows = jnp.zeros((16, ri_cols), local_blocks.dtype)
    meta_rows = meta_rows.at[0, :slot_count].set(pair_list.astype(local_blocks.dtype))
    band_packed = jnp.concatenate([rows2d, meta_rows], axis=0)
    band_ids, band_got = ring_gather(band_packed, "band", band_count)
    xg = jnp.stack(band_got)
    kdim = slot_count * block_size
    codes_g = xg[:, kdim, :slot_count].astype(jnp.float32).astype(jnp.int32)
    grp_ids, grp_got = ring_gather(packed, "grp", group_count)
    xg, *early = lax.optimization_barrier([xg] + grp_got[3:5])
    grp_got[3:5] = early

    occ_cols = lax.dynamic_slice_in_dim(green_occ, band * band_orbs, band_orbs, 1)
    occ_rows = []
    for buf in band_got:
        codes_k = buf[kdim, :slot_count].astype(jnp.float32).astype(jnp.int32)
        row_index = (codes_k // 2)[:, None] * block_size + jnp.arange(block_size, dtype=jnp.int32)
        occ_rows.append(jnp.take(occ_cols, row_index.reshape(-1), axis=0))
    occ_rows = jnp.stack(occ_rows).reshape(band_count, slot_count, block_size, band_orbs)
    halves = (codes_g % 2)[:, None, :] == jnp.arange(2, dtype=jnp.int32)[None, :, None]
    occ_sel = occ_rows[:, None] * halves.astype(occ_rows.dtype)[..., None, None]
    occ_sel = occ_sel.reshape(band_count, 2, kdim, band_orbs)
    occ_raw = jnp.einsum(
        "bkr,bhkl->bhrl", xg[:, :kdim, :], occ_sel, preferred_element_type=jnp.float32
    ).astype(jnp.bfloat16)
    occ_raw = occ_raw.reshape(band_count, 2, block_size, ri_local, band_orbs)
    occ_raw, *later = lax.optimization_barrier([occ_raw] + grp_got[5:7])
    grp_got[5:7] = later

    virt_cols = jnp.concatenate(
        [lax.dynamic_slice_in_dim(green_virt, band_ids[k] * band_orbs, band_orbs, 1) for k in range(band_count)],
        axis=1,
    ).reshape(orbitals, band_count, 2, block_size)
    folded = lax.dot_general(
        occ_raw, virt_cols, (((0, 1, 2), (1, 2, 3)), ((), ())), preferred_element_type=jnp.float32
    )
    xstack = jnp.stack(grp_got)
    codes_b = xstack[:, 0, flat:flat + slot_count].astype(jnp.float32).astype(jnp.int32)
    xrows = xstack.reshape(group_count * ri_local, flat + META)
    arrived = contract(codes_b, folded, xrows, group_count, slot_count, block_size)
    order = jnp.zeros((group_count,), jnp.int32).at[grp_ids].set(jnp.arange(group_count, dtype=jnp.int32))
    arrived = arrived.reshape(ri_local, group_count, ri_local)
    partial_value = jnp.take(arrived, order, axis=1).reshape(ri_local, group_count * ri_local)
    rows_out = ri_local // band_count
    blocks = partial_value.reshape(band_count, rows_out, group_count * ri_local)
    response = lax.dynamic_index_in_dim(blocks, band, 0, keepdims=False)
    for shift in range(1, band_count):
        sent = lax.dynamic_index_in_dim(blocks, (band + shift) % band_count, 0, keepdims=False)
        pairs = [(i, (i + shift) % band_count) for i in range(band_count)]
        response = response + lax.ppermute(sent, "band", pairs)
    return response


def solution(mesh):
    placed = (P("band", None, None, "grp"), P("grp", "band", None), P("grp", "band"), P(), P())
    return jax.shard_map(
        on_device, mesh=mesh, in_specs=placed, out_specs=P(("grp", "band"), None), check_vma=False
    )
```

```python
import jax
import jax.numpy as jnp
from jax import lax
from jax.experimental import pallas as pl
from jax.experimental.pallas import tpu as pltpu
from jax.sharding import PartitionSpec as P

META = 128


def snake(count):
    half = count // 2
    return [2 * o for o in range(half)] + [2 * o + 1 for o in reversed(range(half))]


def ring_gather(buf, axis, count):
    order = snake(count)
    pos_of = [order.index(d) for d in range(count)]
    fwd = [(order[k], order[(k + 1) % count]) for k in range(count)]
    bwd = [(order[k], order[(k - 1) % count]) for k in range(count)]
    me = lax.axis_index(axis)
    pos = jnp.array(pos_of, jnp.int32)[me]
    order_arr = jnp.array(order, jnp.int32)
    shifts = [0]
    got = [buf]
    ahead = behind = buf
    for step in range(1, count // 2):
        ahead = lax.ppermute(ahead, axis, fwd)
        behind = lax.ppermute(behind, axis, bwd)
        got += [ahead, behind]
        shifts += [-step, step]
    rows = buf.shape[0] // 2
    first = lax.ppermute(ahead[:rows], axis, fwd)
    second = lax.ppermute(behind[rows:], axis, bwd)
    got.append(jnp.concatenate([first, second], axis=0))
    shifts.append(count // 2)
    sources = order_arr[(pos + jnp.array(shifts, jnp.int32)) % count]
    return sources, got


def contract_kernel(codes_ref, table_ref, x_ref, out_ref, both_ref, dense_ref, *, slots, width, ri, chunk, blk):
    step = pl.program_id(0)

    @pl.when(step == 0)
    def split():
        lam_count = 2 * blk
        half = both_ref.shape[0] // (2 * ri)
        tiles = table_ref.shape[0] // (ri * lam_count)
        per_tile = 128 // blk
        for h in range(2):
            for j in range(blk):
                for t in range(tiles):
                    lam = h * blk + j
                    start = ((lam // 8) * tiles + t) * 8 + lam % 8
                    rows = table_ref[pl.ds(start, ri, stride=lam_count * tiles), :]
                    hi = rows.astype(jnp.bfloat16)
                    lo = (rows - hi.astype(jnp.float32)).astype(jnp.bfloat16)
                    for u in range(per_tile):
                        code = 2 * (t * per_tile + u) + h
                        both_ref[code * ri:(code + 1) * ri, j * blk:(j + 1) * blk] = hi[:, u * blk:(u + 1) * blk]
                        low = (half + code) * ri
                        both_ref[low:low + ri, j * blk:(j + 1) * blk] = lo[:, u * blk:(u + 1) * blk]

    out_ref[...] = jnp.zeros(out_ref.shape, jnp.float32)
    for s in range(slots):
        xs = x_ref[:, s * width:(s + 1) * width]
        dense = lax.dot_general(
            both_ref[...], xs, (((1,), (1,)), ((), ())), preferred_element_type=jnp.float32
        )
        dense_ref[...] = dense
        for c in range(chunk):
            code = codes_ref[step * chunk + c, s]
            start = pl.multiple_of(code * ri, ri)
            low = pl.multiple_of((code + dense_ref.shape[0] // (2 * ri)) * ri, ri)
            out_ref[0, :, c * ri:(c + 1) * ri] += (
                dense_ref[pl.ds(start, ri), c * ri:(c + 1) * ri] + dense_ref[pl.ds(low, ri), c * ri:(c + 1) * ri]
            )


def contract(codes, folded, xrows, groups, slots, blk):
    ri, lam_count, orbitals = folded.shape
    width = blk * blk
    codes_total = 2 * (orbitals // blk)
    flat = slots * width
    chunk = groups
    while chunk > 1 and (chunk * ri * flat * 2 > (4 << 20) or groups % chunk):
        chunk -= 1
    steps = groups // chunk
    tiles = orbitals // 128
    table2 = folded.reshape(ri, lam_count // 8, 8, tiles, 128)
    table2 = jnp.transpose(table2, (0, 1, 3, 2, 4)).reshape(ri * lam_count * tiles, 128)
    grid_spec = pltpu.PrefetchScalarGridSpec(
        num_scalar_prefetch=1,
        grid=(steps,),
        in_specs=[
            pl.BlockSpec(table2.shape, lambda g, c: (0, 0)),
            pl.BlockSpec((chunk * ri, flat), lambda g, c: (g, 0)),
        ],
        out_specs=pl.BlockSpec((1, ri, chunk * ri), lambda g, c: (g, 0, 0)),
        scratch_shapes=[
            pltpu.VMEM((2 * codes_total * ri, width), jnp.bfloat16),
            pltpu.VMEM((2 * codes_total * ri, chunk * ri), jnp.float32),
        ],
    )
    body = lambda *refs: contract_kernel(*refs, slots=slots, width=width, ri=ri, chunk=chunk, blk=blk)
    out = pl.pallas_call(
        body, out_shape=jax.ShapeDtypeStruct((steps, ri, chunk * ri), jnp.float32), grid_spec=grid_spec
    )(codes, table2, xrows)
    return jnp.transpose(out, (1, 0, 2)).reshape(ri, groups * ri)


def on_device(x_blocks, pair_ids, live_count, green_occ, green_virt):
    local_blocks = x_blocks[0]
    slot_count, block_size, ri_cols = local_blocks.shape
    ri_local = ri_cols // block_size
    orbitals = green_occ.shape[0]
    band_orbs = 2 * block_size
    band_count = lax.axis_size("band")
    group_count = lax.axis_size("grp")
    band = lax.axis_index("band")
    flat = slot_count * block_size * block_size
    code_count = 2 * (orbitals // block_size)

    pair_list = pair_ids[0, 0]
    live_slots = live_count[0, 0]

    live = (jnp.arange(slot_count, dtype=jnp.int32) < live_slots).astype(local_blocks.dtype)
    masked = local_blocks * live[:, None, None]
    xt = masked.reshape(slot_count, block_size, ri_local, block_size)
    xt = jnp.transpose(xt, (2, 0, 3, 1)).reshape(ri_local, flat)
    meta = jnp.zeros((ri_local, META), local_blocks.dtype)
    meta = meta.at[0, :slot_count].set(pair_list.astype(local_blocks.dtype))
    packed = jnp.concatenate([xt, meta], axis=1)

    grp_ids, grp_got = ring_gather(packed, "grp", group_count)
    rows2d = masked.reshape(slot_count, block_size, ri_local, block_size)
    rows2d = jnp.transpose(rows2d, (0, 1, 3, 2)).reshape(slot_count * block_size, ri_cols)
    meta_rows = jnp.zeros((16, ri_cols), local_blocks.dtype)
    meta_rows = meta_rows.at[0, :slot_count].set(pair_list.astype(local_blocks.dtype))
    band_packed = jnp.concatenate([rows2d, meta_rows], axis=0)
    band_ids, band_got = ring_gather(band_packed, "band", band_count)
    xg = jnp.stack(band_got)
    kdim = slot_count * block_size
    codes_g = xg[:, kdim, :slot_count].astype(jnp.float32).astype(jnp.int32)
    xg, *early = lax.optimization_barrier([xg] + grp_got[3:5])
    grp_got[3:5] = early

    occ_cols = lax.dynamic_slice_in_dim(green_occ, band * band_orbs, band_orbs, 1)
    row_index = (codes_g // 2)[..., None] * block_size + jnp.arange(block_size, dtype=jnp.int32)
    occ_rows = jnp.take(occ_cols, row_index.reshape(-1), axis=0)
    occ_rows = occ_rows.reshape(band_count, slot_count, block_size, band_orbs)
    halves = (codes_g % 2)[:, None, :] == jnp.arange(2, dtype=jnp.int32)[None, :, None]
    occ_sel = occ_rows[:, None] * halves.astype(occ_rows.dtype)[..., None, None]
    occ_sel = occ_sel.reshape(band_count, 2, kdim, band_orbs)
    occ_raw = jnp.einsum(
        "bkr,bhkl->bhrl", xg[:, :kdim, :], occ_sel, preferred_element_type=jnp.float32
    ).astype(jnp.bfloat16)
    occ_raw = occ_raw.reshape(band_count, 2, block_size, ri_local, band_orbs)
    occ_raw, *later = lax.optimization_barrier([occ_raw] + grp_got[5:7])
    grp_got[5:7] = later

    virt_cols = jnp.concatenate(
        [lax.dynamic_slice_in_dim(green_virt, band_ids[k] * band_orbs, band_orbs, 1) for k in range(band_count)],
        axis=1,
    ).reshape(orbitals, band_count, 2, block_size)
    folded = lax.dot_general(
        occ_raw, virt_cols, (((0, 1, 2), (1, 2, 3)), ((), ())), preferred_element_type=jnp.float32
    )
    xstack = jnp.stack(grp_got)
    codes_b = xstack[:, 0, flat:flat + slot_count].astype(jnp.float32).astype(jnp.int32)
    xrows = xstack.reshape(group_count * ri_local, flat + META)
    arrived = contract(codes_b, folded, xrows, group_count, slot_count, block_size)
    order = jnp.zeros((group_count,), jnp.int32).at[grp_ids].set(jnp.arange(group_count, dtype=jnp.int32))
    arrived = arrived.reshape(ri_local, group_count, ri_local)
    partial_value = jnp.take(arrived, order, axis=1).reshape(ri_local, group_count * ri_local)
    rows_out = ri_local // band_count
    blocks = partial_value.reshape(band_count, rows_out, group_count * ri_local)
    response = lax.dynamic_index_in_dim(blocks, band, 0, keepdims=False)
    for shift in range(1, band_count):
        sent = lax.dynamic_index_in_dim(blocks, (band + shift) % band_count, 0, keepdims=False)
        pairs = [(i, (i + shift) % band_count) for i in range(band_count)]
        response = response + lax.ppermute(sent, "band", pairs)
    return response


def solution(mesh):
    placed = (P("band", None, None, "grp"), P("grp", "band", None), P("grp", "band"), P(), P())
    return jax.shard_map(
        on_device, mesh=mesh, in_specs=placed, out_specs=P(("grp", "band"), None), check_vma=False
    )
```

```python
import jax
import jax.numpy as jnp
from jax import lax
from jax.experimental import pallas as pl
from jax.experimental.pallas import tpu as pltpu
from jax.sharding import PartitionSpec as P

META = 128


def snake(count):
    half = count // 2
    return [2 * o for o in range(half)] + [2 * o + 1 for o in reversed(range(half))]


def ring_gather(buf, axis, count):
    order = snake(count)
    pos_of = [order.index(d) for d in range(count)]
    fwd = [(order[k], order[(k + 1) % count]) for k in range(count)]
    bwd = [(order[k], order[(k - 1) % count]) for k in range(count)]
    me = lax.axis_index(axis)
    pos = jnp.array(pos_of, jnp.int32)[me]
    order_arr = jnp.array(order, jnp.int32)
    shifts = [0]
    got = [buf]
    ahead = behind = buf
    for step in range(1, count // 2):
        ahead = lax.ppermute(ahead, axis, fwd)
        behind = lax.ppermute(behind, axis, bwd)
        got += [ahead, behind]
        shifts += [-step, step]
    rows = buf.shape[0] // 2
    first = lax.ppermute(ahead[:rows], axis, fwd)
    second = lax.ppermute(behind[rows:], axis, bwd)
    got.append(jnp.concatenate([first, second], axis=0))
    shifts.append(count // 2)
    sources = order_arr[(pos + jnp.array(shifts, jnp.int32)) % count]
    return sources, got


def contract_kernel(codes_ref, table_ref, x_ref, out_ref, both_ref, dense_ref, *, slots, width, ri, chunk, blk):
    step = pl.program_id(0)
    s = pl.program_id(1)

    @pl.when(jnp.logical_and(step == 0, s == 0))
    def split():
        lam_count = 2 * blk
        half = both_ref.shape[0] // (2 * ri)
        tiles = table_ref.shape[0] // (ri * lam_count)
        per_tile = 128 // blk
        for h in range(2):
            for j in range(blk):
                for t in range(tiles):
                    lam = h * blk + j
                    start = ((lam // 8) * tiles + t) * 8 + lam % 8
                    rows = table_ref[pl.ds(start, ri, stride=lam_count * tiles), :]
                    hi = rows.astype(jnp.bfloat16)
                    lo = (rows - hi.astype(jnp.float32)).astype(jnp.bfloat16)
                    for u in range(per_tile):
                        code = 2 * (t * per_tile + u) + h
                        both_ref[code * ri:(code + 1) * ri, j * blk:(j + 1) * blk] = hi[:, u * blk:(u + 1) * blk]
                        low = (half + code) * ri
                        both_ref[low:low + ri, j * blk:(j + 1) * blk] = lo[:, u * blk:(u + 1) * blk]

    @pl.when(s == 0)
    def clear():
        out_ref[...] = jnp.zeros(out_ref.shape, jnp.float32)

    dense_ref[...] = lax.dot_general(
        both_ref[...], x_ref[...], (((1,), (1,)), ((), ())), preferred_element_type=jnp.float32
    )
    for c in range(chunk):
        code = codes_ref[step * chunk + c, s]
        start = pl.multiple_of(code * ri, ri)
        low = pl.multiple_of((code + dense_ref.shape[0] // (2 * ri)) * ri, ri)
        out_ref[0, :, c * ri:(c + 1) * ri] += (
            dense_ref[pl.ds(start, ri), c * ri:(c + 1) * ri] + dense_ref[pl.ds(low, ri), c * ri:(c + 1) * ri]
        )


def contract(codes, folded, xrows, groups, slots, blk):
    ri, lam_count, orbitals = folded.shape
    width = blk * blk
    codes_total = 2 * (orbitals // blk)
    flat = slots * width
    chunk = groups
    while chunk > 1 and (chunk * ri * flat * 2 > (4 << 20) or groups % chunk):
        chunk -= 1
    steps = groups // chunk
    tiles = orbitals // 128
    table2 = folded.reshape(ri, lam_count // 8, 8, tiles, 128)
    table2 = jnp.transpose(table2, (0, 1, 3, 2, 4)).reshape(ri * lam_count * tiles, 128)
    grid_spec = pltpu.PrefetchScalarGridSpec(
        num_scalar_prefetch=1,
        grid=(steps, slots),
        in_specs=[
            pl.BlockSpec(table2.shape, lambda g, s, c: (0, 0)),
            pl.BlockSpec((chunk * ri, width), lambda g, s, c: (g, s)),
        ],
        out_specs=pl.BlockSpec((1, ri, chunk * ri), lambda g, s, c: (g, 0, 0)),
        scratch_shapes=[
            pltpu.VMEM((2 * codes_total * ri, width), jnp.bfloat16),
            pltpu.VMEM((2 * codes_total * ri, chunk * ri), jnp.float32),
        ],
    )
    body = lambda *refs: contract_kernel(*refs, slots=slots, width=width, ri=ri, chunk=chunk, blk=blk)
    out = pl.pallas_call(
        body, out_shape=jax.ShapeDtypeStruct((steps, ri, chunk * ri), jnp.float32), grid_spec=grid_spec
    )(codes, table2, xrows)
    return jnp.transpose(out, (1, 0, 2)).reshape(ri, groups * ri)


def on_device(x_blocks, pair_ids, live_count, green_occ, green_virt):
    local_blocks = x_blocks[0]
    slot_count, block_size, ri_cols = local_blocks.shape
    ri_local = ri_cols // block_size
    orbitals = green_occ.shape[0]
    band_orbs = 2 * block_size
    band_count = lax.axis_size("band")
    group_count = lax.axis_size("grp")
    band = lax.axis_index("band")
    flat = slot_count * block_size * block_size
    code_count = 2 * (orbitals // block_size)

    pair_list = pair_ids[0, 0]
    live_slots = live_count[0, 0]

    live = (jnp.arange(slot_count, dtype=jnp.int32) < live_slots).astype(local_blocks.dtype)
    masked = local_blocks * live[:, None, None]
    xt = masked.reshape(slot_count, block_size, ri_local, block_size)
    xt = jnp.transpose(xt, (2, 0, 3, 1)).reshape(ri_local, flat)
    meta = jnp.zeros((ri_local, META), local_blocks.dtype)
    meta = meta.at[0, :slot_count].set(pair_list.astype(local_blocks.dtype))
    packed = jnp.concatenate([xt, meta], axis=1)

    grp_ids, grp_got = ring_gather(packed, "grp", group_count)
    rows2d = masked.reshape(slot_count, block_size, ri_local, block_size)
    rows2d = jnp.transpose(rows2d, (0, 1, 3, 2)).reshape(slot_count * block_size, ri_cols)
    meta_rows = jnp.zeros((16, ri_cols), local_blocks.dtype)
    meta_rows = meta_rows.at[0, :slot_count].set(pair_list.astype(local_blocks.dtype))
    band_packed = jnp.concatenate([rows2d, meta_rows], axis=0)
    band_ids, band_got = ring_gather(band_packed, "band", band_count)
    xg = jnp.stack(band_got)
    kdim = slot_count * block_size
    codes_g = xg[:, kdim, :slot_count].astype(jnp.float32).astype(jnp.int32)
    xg, *early = lax.optimization_barrier([xg] + grp_got[3:5])
    grp_got[3:5] = early

    occ_cols = lax.dynamic_slice_in_dim(green_occ, band * band_orbs, band_orbs, 1)
    row_index = (codes_g // 2)[..., None] * block_size + jnp.arange(block_size, dtype=jnp.int32)
    occ_rows = jnp.take(occ_cols, row_index.reshape(-1), axis=0)
    occ_rows = occ_rows.reshape(band_count, slot_count, block_size, band_orbs)
    halves = (codes_g % 2)[:, None, :] == jnp.arange(2, dtype=jnp.int32)[None, :, None]
    occ_sel = occ_rows[:, None] * halves.astype(occ_rows.dtype)[..., None, None]
    occ_sel = occ_sel.reshape(band_count, 2, kdim, band_orbs)
    occ_raw = jnp.einsum(
        "bkr,bhkl->bhrl", xg[:, :kdim, :], occ_sel, preferred_element_type=jnp.float32
    ).astype(jnp.bfloat16)
    occ_raw = occ_raw.reshape(band_count, 2, block_size, ri_local, band_orbs)
    occ_raw, *later = lax.optimization_barrier([occ_raw] + grp_got[5:7])
    grp_got[5:7] = later

    virt_cols = jnp.concatenate(
        [lax.dynamic_slice_in_dim(green_virt, band_ids[k] * band_orbs, band_orbs, 1) for k in range(band_count)],
        axis=1,
    ).reshape(orbitals, band_count, 2, block_size)
    folded = lax.dot_general(
        occ_raw, virt_cols, (((0, 1, 2), (1, 2, 3)), ((), ())), preferred_element_type=jnp.float32
    )
    xstack = jnp.stack(grp_got)
    codes_b = xstack[:, 0, flat:flat + slot_count].astype(jnp.float32).astype(jnp.int32)
    xrows = xstack.reshape(group_count * ri_local, flat + META)
    arrived = contract(codes_b, folded, xrows, group_count, slot_count, block_size)
    order = jnp.zeros((group_count,), jnp.int32).at[grp_ids].set(jnp.arange(group_count, dtype=jnp.int32))
    arrived = arrived.reshape(ri_local, group_count, ri_local)
    partial_value = jnp.take(arrived, order, axis=1).reshape(ri_local, group_count * ri_local)
    rows_out = ri_local // band_count
    blocks = partial_value.reshape(band_count, rows_out, group_count * ri_local)
    response = lax.dynamic_index_in_dim(blocks, band, 0, keepdims=False)
    for shift in range(1, band_count):
        sent = lax.dynamic_index_in_dim(blocks, (band + shift) % band_count, 0, keepdims=False)
        pairs = [(i, (i + shift) % band_count) for i in range(band_count)]
        response = response + lax.ppermute(sent, "band", pairs)
    return response


def solution(mesh):
    placed = (P("band", None, None, "grp"), P("grp", "band", None), P("grp", "band"), P(), P())
    return jax.shard_map(
        on_device, mesh=mesh, in_specs=placed, out_specs=P(("grp", "band"), None), check_vma=False
    )
```

```python
import jax
import jax.numpy as jnp
from jax import lax
from jax.experimental import pallas as pl
from jax.experimental.pallas import tpu as pltpu
from jax.sharding import PartitionSpec as P

META = 128


def snake(count):
    half = count // 2
    return [2 * o for o in range(half)] + [2 * o + 1 for o in reversed(range(half))]


def ring_gather(buf, axis, count):
    order = snake(count)
    pos_of = [order.index(d) for d in range(count)]
    fwd = [(order[k], order[(k + 1) % count]) for k in range(count)]
    bwd = [(order[k], order[(k - 1) % count]) for k in range(count)]
    me = lax.axis_index(axis)
    pos = jnp.array(pos_of, jnp.int32)[me]
    order_arr = jnp.array(order, jnp.int32)
    shifts = [0]
    got = [buf]
    ahead = behind = buf
    for step in range(1, count // 2):
        ahead = lax.ppermute(ahead, axis, fwd)
        behind = lax.ppermute(behind, axis, bwd)
        got += [ahead, behind]
        shifts += [-step, step]
    cols = (buf.shape[1] // 256) * 128
    first = lax.ppermute(ahead[:, :cols], axis, fwd)
    second = lax.ppermute(behind[:, cols:], axis, bwd)
    got.append(jnp.concatenate([first, second], axis=1))
    shifts.append(count // 2)
    sources = order_arr[(pos + jnp.array(shifts, jnp.int32)) % count]
    return sources, got


def contract_kernel(codes_ref, table_ref, x_ref, out_ref, both_ref, dense_ref, *, slots, width, ri, chunk, blk):
    step = pl.program_id(0)

    @pl.when(step == 0)
    def split():
        lam_count = 2 * blk
        half = both_ref.shape[0] // (2 * ri)
        tiles = table_ref.shape[0] // (ri * lam_count)
        per_tile = 128 // blk
        for h in range(2):
            for j in range(blk):
                for t in range(tiles):
                    lam = h * blk + j
                    start = ((lam // 8) * tiles + t) * 8 + lam % 8
                    rows = table_ref[pl.ds(start, ri, stride=lam_count * tiles), :]
                    hi = rows.astype(jnp.bfloat16)
                    lo = (rows - hi.astype(jnp.float32)).astype(jnp.bfloat16)
                    for u in range(per_tile):
                        code = 2 * (t * per_tile + u) + h
                        both_ref[code * ri:(code + 1) * ri, j * blk:(j + 1) * blk] = hi[:, u * blk:(u + 1) * blk]
                        low = (half + code) * ri
                        both_ref[low:low + ri, j * blk:(j + 1) * blk] = lo[:, u * blk:(u + 1) * blk]

    out_ref[...] = jnp.zeros(out_ref.shape, jnp.float32)
    for s in range(slots):
        xs = x_ref[:, s * width:(s + 1) * width]
        dense = lax.dot_general(
            both_ref[...], xs, (((1,), (1,)), ((), ())), preferred_element_type=jnp.float32
        )
        dense_ref[...] = dense
        for c in range(chunk):
            code = codes_ref[step * chunk + c, s]
            start = pl.multiple_of(code * ri, ri)
            low = pl.multiple_of((code + dense_ref.shape[0] // (2 * ri)) * ri, ri)
            out_ref[0, :, c * ri:(c + 1) * ri] += (
                dense_ref[pl.ds(start, ri), c * ri:(c + 1) * ri] + dense_ref[pl.ds(low, ri), c * ri:(c + 1) * ri]
            )


def contract(codes, folded, xrows, groups, slots, blk):
    ri, lam_count, orbitals = folded.shape
    width = blk * blk
    codes_total = 2 * (orbitals // blk)
    flat = slots * width
    chunk = groups
    while chunk > 1 and (chunk * ri * flat * 2 > (4 << 20) or groups % chunk):
        chunk -= 1
    steps = groups // chunk
    tiles = orbitals // 128
    table2 = folded.reshape(ri, lam_count // 8, 8, tiles, 128)
    table2 = jnp.transpose(table2, (0, 1, 3, 2, 4)).reshape(ri * lam_count * tiles, 128)
    grid_spec = pltpu.PrefetchScalarGridSpec(
        num_scalar_prefetch=1,
        grid=(steps,),
        in_specs=[
            pl.BlockSpec(table2.shape, lambda g, c: (0, 0)),
            pl.BlockSpec((chunk * ri, flat), lambda g, c: (g, 0)),
        ],
        out_specs=pl.BlockSpec((1, ri, chunk * ri), lambda g, c: (g, 0, 0)),
        scratch_shapes=[
            pltpu.VMEM((2 * codes_total * ri, width), jnp.bfloat16),
            pltpu.VMEM((2 * codes_total * ri, chunk * ri), jnp.float32),
        ],
    )
    body = lambda *refs: contract_kernel(*refs, slots=slots, width=width, ri=ri, chunk=chunk, blk=blk)
    out = pl.pallas_call(
        body, out_shape=jax.ShapeDtypeStruct((steps, ri, chunk * ri), jnp.float32), grid_spec=grid_spec
    )(codes, table2, xrows)
    return jnp.transpose(out, (1, 0, 2)).reshape(ri, groups * ri)


def on_device(x_blocks, pair_ids, live_count, green_occ, green_virt):
    local_blocks = x_blocks[0]
    slot_count, block_size, ri_cols = local_blocks.shape
    ri_local = ri_cols // block_size
    orbitals = green_occ.shape[0]
    band_orbs = 2 * block_size
    band_count = lax.axis_size("band")
    group_count = lax.axis_size("grp")
    band = lax.axis_index("band")
    flat = slot_count * block_size * block_size
    code_count = 2 * (orbitals // block_size)

    pair_list = pair_ids[0, 0]
    live_slots = live_count[0, 0]

    live = (jnp.arange(slot_count, dtype=jnp.int32) < live_slots).astype(local_blocks.dtype)
    masked = local_blocks * live[:, None, None]
    xt = masked.reshape(slot_count, block_size, ri_local, block_size)
    xt = jnp.transpose(xt, (2, 0, 3, 1)).reshape(ri_local, flat)
    meta = jnp.zeros((ri_local, META), local_blocks.dtype)
    meta = meta.at[0, :slot_count].set(pair_list.astype(local_blocks.dtype))
    packed = jnp.concatenate([xt, meta], axis=1)

    grp_ids, grp_got = ring_gather(packed, "grp", group_count)
    rows2d = masked.reshape(slot_count, block_size, ri_local, block_size)
    rows2d = jnp.transpose(rows2d, (0, 1, 3, 2)).reshape(slot_count * block_size, ri_cols)
    meta_rows = jnp.zeros((16, ri_cols), local_blocks.dtype)
    meta_rows = meta_rows.at[0, :slot_count].set(pair_list.astype(local_blocks.dtype))
    band_packed = jnp.concatenate([rows2d, meta_rows], axis=0)
    band_ids, band_got = ring_gather(band_packed, "band", band_count)
    xg = jnp.stack(band_got)
    kdim = slot_count * block_size
    codes_g = xg[:, kdim, :slot_count].astype(jnp.float32).astype(jnp.int32)
    xg, *early = lax.optimization_barrier([xg] + grp_got[3:5])
    grp_got[3:5] = early

    occ_cols = lax.dynamic_slice_in_dim(green_occ, band * band_orbs, band_orbs, 1)
    row_index = (codes_g // 2)[..., None] * block_size + jnp.arange(block_size, dtype=jnp.int32)
    occ_rows = jnp.take(occ_cols, row_index.reshape(-1), axis=0)
    occ_rows = occ_rows.reshape(band_count, slot_count, block_size, band_orbs)
    halves = (codes_g % 2)[:, None, :] == jnp.arange(2, dtype=jnp.int32)[None, :, None]
    occ_sel = occ_rows[:, None] * halves.astype(occ_rows.dtype)[..., None, None]
    occ_sel = occ_sel.reshape(band_count, 2, kdim, band_orbs)
    occ_raw = jnp.einsum(
        "bkr,bhkl->bhrl", xg[:, :kdim, :], occ_sel, preferred_element_type=jnp.float32
    ).astype(jnp.bfloat16)
    occ_raw = occ_raw.reshape(band_count, 2, block_size, ri_local, band_orbs)
    occ_raw, *later = lax.optimization_barrier([occ_raw] + grp_got[5:7])
    grp_got[5:7] = later

    virt_cols = jnp.concatenate(
        [lax.dynamic_slice_in_dim(green_virt, band_ids[k] * band_orbs, band_orbs, 1) for k in range(band_count)],
        axis=1,
    ).reshape(orbitals, band_count, 2, block_size)
    folded = lax.dot_general(
        occ_raw, virt_cols, (((0, 1, 2), (1, 2, 3)), ((), ())), preferred_element_type=jnp.float32
    )
    xstack = jnp.stack(grp_got)
    codes_b = xstack[:, 0, flat:flat + slot_count].astype(jnp.float32).astype(jnp.int32)
    xrows = xstack.reshape(group_count * ri_local, flat + META)
    arrived = contract(codes_b, folded, xrows, group_count, slot_count, block_size)
    order = jnp.zeros((group_count,), jnp.int32).at[grp_ids].set(jnp.arange(group_count, dtype=jnp.int32))
    arrived = arrived.reshape(ri_local, group_count, ri_local)
    partial_value = jnp.take(arrived, order, axis=1).reshape(ri_local, group_count * ri_local)
    rows_out = ri_local // band_count
    blocks = partial_value.reshape(band_count, rows_out, group_count * ri_local)
    response = lax.dynamic_index_in_dim(blocks, band, 0, keepdims=False)
    for shift in range(1, band_count):
        sent = lax.dynamic_index_in_dim(blocks, (band + shift) % band_count, 0, keepdims=False)
        pairs = [(i, (i + shift) % band_count) for i in range(band_count)]
        response = response + lax.ppermute(sent, "band", pairs)
    return response


def solution(mesh):
    placed = (P("band", None, None, "grp"), P("grp", "band", None), P("grp", "band"), P(), P())
    return jax.shard_map(
        on_device, mesh=mesh, in_specs=placed, out_specs=P(("grp", "band"), None), check_vma=False
    )
```

```python
import jax
import jax.numpy as jnp
from jax import lax
from jax.experimental import pallas as pl
from jax.experimental.pallas import tpu as pltpu
from jax.sharding import PartitionSpec as P

META = 128


def snake(count):
    half = count // 2
    return [2 * o for o in range(half)] + [2 * o + 1 for o in reversed(range(half))]


def ring_gather(buf, axis, count):
    order = snake(count)
    pos_of = [order.index(d) for d in range(count)]
    fwd = [(order[k], order[(k + 1) % count]) for k in range(count)]
    bwd = [(order[k], order[(k - 1) % count]) for k in range(count)]
    me = lax.axis_index(axis)
    pos = jnp.array(pos_of, jnp.int32)[me]
    order_arr = jnp.array(order, jnp.int32)
    shifts = [0]
    got = [buf]
    ahead = behind = buf
    for step in range(1, count // 2):
        ahead = lax.ppermute(ahead, axis, fwd)
        behind = lax.ppermute(behind, axis, bwd)
        got += [ahead, behind]
        shifts += [-step, step]
    rows = (buf.shape[0] // 32) * 16 if buf.shape[0] >= 32 else buf.shape[0] // 2
    first = lax.ppermute(ahead[:rows], axis, fwd)
    second = lax.ppermute(behind[rows:], axis, bwd)
    got.append(jnp.concatenate([first, second], axis=0))
    shifts.append(count // 2)
    sources = order_arr[(pos + jnp.array(shifts, jnp.int32)) % count]
    return sources, got


def contract_kernel(codes_ref, table_ref, x_ref, out_ref, both_ref, dense_ref, *, slots, width, ri, chunk, blk):
    step = pl.program_id(0)

    @pl.when(step == 0)
    def split():
        lam_count = 2 * blk
        half = both_ref.shape[0] // (2 * ri)
        tiles = table_ref.shape[0] // (ri * lam_count)
        per_tile = 128 // blk
        for h in range(2):
            for j in range(blk):
                for t in range(tiles):
                    lam = h * blk + j
                    start = ((lam // 8) * tiles + t) * 8 + lam % 8
                    rows = table_ref[pl.ds(start, ri, stride=lam_count * tiles), :]
                    hi = rows.astype(jnp.bfloat16)
                    lo = (rows - hi.astype(jnp.float32)).astype(jnp.bfloat16)
                    for u in range(per_tile):
                        code = 2 * (t * per_tile + u) + h
                        both_ref[code * ri:(code + 1) * ri, j * blk:(j + 1) * blk] = hi[:, u * blk:(u + 1) * blk]
                        low = (half + code) * ri
                        both_ref[low:low + ri, j * blk:(j + 1) * blk] = lo[:, u * blk:(u + 1) * blk]

    out_ref[...] = jnp.zeros(out_ref.shape, jnp.float32)
    for s in range(slots):
        xs = x_ref[:, s * width:(s + 1) * width]
        dense = lax.dot_general(
            both_ref[...], xs, (((1,), (1,)), ((), ())), preferred_element_type=jnp.float32
        )
        dense_ref[...] = dense
        for c in range(chunk):
            code = codes_ref[step * chunk + c, s]
            start = pl.multiple_of(code * ri, ri)
            low = pl.multiple_of((code + dense_ref.shape[0] // (2 * ri)) * ri, ri)
            out_ref[0, :, c * ri:(c + 1) * ri] += (
                dense_ref[pl.ds(start, ri), c * ri:(c + 1) * ri] + dense_ref[pl.ds(low, ri), c * ri:(c + 1) * ri]
            )


def contract(codes, folded, xrows, groups, slots, blk):
    ri, lam_count, orbitals = folded.shape
    width = blk * blk
    codes_total = 2 * (orbitals // blk)
    flat = slots * width
    chunk = groups
    while chunk > 1 and (chunk * ri * flat * 2 > (4 << 20) or groups % chunk):
        chunk -= 1
    steps = groups // chunk
    tiles = orbitals // 128
    table2 = folded.reshape(ri, lam_count // 8, 8, tiles, 128)
    table2 = jnp.transpose(table2, (0, 1, 3, 2, 4)).reshape(ri * lam_count * tiles, 128)
    grid_spec = pltpu.PrefetchScalarGridSpec(
        num_scalar_prefetch=1,
        grid=(steps,),
        in_specs=[
            pl.BlockSpec(table2.shape, lambda g, c: (0, 0)),
            pl.BlockSpec((chunk * ri, flat), lambda g, c: (g, 0)),
        ],
        out_specs=pl.BlockSpec((1, ri, chunk * ri), lambda g, c: (g, 0, 0)),
        scratch_shapes=[
            pltpu.VMEM((2 * codes_total * ri, width), jnp.bfloat16),
            pltpu.VMEM((2 * codes_total * ri, chunk * ri), jnp.float32),
        ],
    )
    body = lambda *refs: contract_kernel(*refs, slots=slots, width=width, ri=ri, chunk=chunk, blk=blk)
    out = pl.pallas_call(
        body, out_shape=jax.ShapeDtypeStruct((steps, ri, chunk * ri), jnp.float32), grid_spec=grid_spec
    )(codes, table2, xrows)
    return jnp.transpose(out, (1, 0, 2)).reshape(ri, groups * ri)


def on_device(x_blocks, pair_ids, live_count, green_occ, green_virt):
    local_blocks = x_blocks[0]
    slot_count, block_size, ri_cols = local_blocks.shape
    ri_local = ri_cols // block_size
    orbitals = green_occ.shape[0]
    band_orbs = 2 * block_size
    band_count = lax.axis_size("band")
    group_count = lax.axis_size("grp")
    band = lax.axis_index("band")
    flat = slot_count * block_size * block_size
    code_count = 2 * (orbitals // block_size)

    pair_list = pair_ids[0, 0]
    live_slots = live_count[0, 0]

    live = (jnp.arange(slot_count, dtype=jnp.int32) < live_slots).astype(local_blocks.dtype)
    masked = local_blocks * live[:, None, None]
    xt = masked.reshape(slot_count, block_size, ri_local, block_size)
    xt = jnp.transpose(xt, (2, 0, 3, 1)).reshape(ri_local, flat)
    meta = jnp.zeros((ri_local, META), local_blocks.dtype)
    meta = meta.at[0, :slot_count].set(pair_list.astype(local_blocks.dtype))
    packed = jnp.concatenate([xt, meta], axis=1)

    grp_ids, grp_got = ring_gather(packed, "grp", group_count)
    rows2d = masked.reshape(slot_count, block_size, ri_local, block_size)
    rows2d = jnp.transpose(rows2d, (0, 1, 3, 2)).reshape(slot_count * block_size, ri_cols)
    meta_rows = jnp.zeros((16, ri_cols), local_blocks.dtype)
    meta_rows = meta_rows.at[0, :slot_count].set(pair_list.astype(local_blocks.dtype))
    band_packed = jnp.concatenate([rows2d, meta_rows], axis=0)
    band_ids, band_got = ring_gather(band_packed, "band", band_count)
    xg = jnp.stack(band_got)
    kdim = slot_count * block_size
    codes_g = xg[:, kdim, :slot_count].astype(jnp.float32).astype(jnp.int32)
    xg, *early = lax.optimization_barrier([xg] + grp_got[3:5])
    grp_got[3:5] = early

    occ_cols = lax.dynamic_slice_in_dim(green_occ, band * band_orbs, band_orbs, 1)
    row_index = (codes_g // 2)[..., None] * block_size + jnp.arange(block_size, dtype=jnp.int32)
    occ_rows = jnp.take(occ_cols, row_index.reshape(-1), axis=0)
    occ_rows = occ_rows.reshape(band_count, slot_count, block_size, band_orbs)
    halves = (codes_g % 2)[:, None, :] == jnp.arange(2, dtype=jnp.int32)[None, :, None]
    occ_sel = occ_rows[:, None] * halves.astype(occ_rows.dtype)[..., None, None]
    occ_sel = occ_sel.reshape(band_count, 2, kdim, band_orbs)
    occ_raw = jnp.einsum(
        "bkr,bhkl->bhrl", xg[:, :kdim, :], occ_sel, preferred_element_type=jnp.float32
    ).astype(jnp.bfloat16)
    occ_raw = occ_raw.reshape(band_count, 2, block_size, ri_local, band_orbs)
    occ_raw, *later = lax.optimization_barrier([occ_raw] + grp_got[5:7])
    grp_got[5:7] = later

    virt_cols = jnp.concatenate(
        [lax.dynamic_slice_in_dim(green_virt, band_ids[k] * band_orbs, band_orbs, 1) for k in range(band_count)],
        axis=1,
    ).reshape(orbitals, band_count, 2, block_size)
    folded = lax.dot_general(
        occ_raw, virt_cols, (((0, 1, 2), (1, 2, 3)), ((), ())), preferred_element_type=jnp.float32
    )
    xstack = jnp.stack(grp_got)
    codes_b = xstack[:, 0, flat:flat + slot_count].astype(jnp.float32).astype(jnp.int32)
    xrows = xstack.reshape(group_count * ri_local, flat + META)
    arrived = contract(codes_b, folded, xrows, group_count, slot_count, block_size)
    order = jnp.zeros((group_count,), jnp.int32).at[grp_ids].set(jnp.arange(group_count, dtype=jnp.int32))
    arrived = arrived.reshape(ri_local, group_count, ri_local)
    partial_value = jnp.take(arrived, order, axis=1).reshape(ri_local, group_count * ri_local)
    rows_out = ri_local // band_count
    blocks = partial_value.reshape(band_count, rows_out, group_count * ri_local)
    response = lax.dynamic_index_in_dim(blocks, band, 0, keepdims=False)
    for shift in range(1, band_count):
        sent = lax.dynamic_index_in_dim(blocks, (band + shift) % band_count, 0, keepdims=False)
        pairs = [(i, (i + shift) % band_count) for i in range(band_count)]
        response = response + lax.ppermute(sent, "band", pairs)
    return response


def solution(mesh):
    placed = (P("band", None, None, "grp"), P("grp", "band", None), P("grp", "band"), P(), P())
    return jax.shard_map(
        on_device, mesh=mesh, in_specs=placed, out_specs=P(("grp", "band"), None), check_vma=False
    )
```
